256 devices in a mesh: kv: 8 (over x, core), seq: 32 (over z, y).
Axes of the slice: x: 4, y: 4, z: 8, core: 2. Of those that a mesh axis runs over, the one named last changes fastest.
Arguments:
- hidden_states: bfloat16 [6144, 2048], P('seq')
- attn_gain: float32 [2048], replicated, may hold values from 0.5 to 1.5
- w_q: bfloat16 [2048, 2048], P(None, 'kv')
- w_k: bfloat16 [2048, 512], P(None, 'kv')
- w_v: bfloat16 [2048, 512], P(None, 'kv'), may hold values from -0.125 to 0.125
- w_o: bfloat16 [2048, 2048], P('kv'), may hold values from -0.125 to 0.125
- final_gain: float32 [2048], replicated, may hold values from 0.5 to 1.5
- w_head: bfloat16 [2048, 49408], P(None, ('kv', 'seq'))
- doc_lengths: int32 [26], replicated, may hold values from 1 to 3072, as said below
- target_ids: int32 [6144], replicated, may hold values from 0 to 49154, as said below
- vocab_mask: int32 [49408], P(('kv', 'seq')), may hold values from 0 to 1, as said below
Outputs:
- log_probs: float32 [6144], P('seq')
- entropies: float32 [6144], P('seq')
The draws below stay inside these ranges and needn't reach their ends.
Inputs may be any that keep to these rules, and one draw needn't show every extreme that they name: `doc_lengths`: they sum to 6144; one is 3072, one more is over 1536, every other is under 64. `target_ids`: each names an entry whose vocab_mask is 1. `vocab_mask`: entries from 49155 on are 0.
All inputs are finite; a program needn't handle non-finite values.
Results may differ from the reference program's by a relative error of at most 0.0045.
Values may be sent and summed in bfloat16 or wider, within the bound.
No kernel may reach another device: no remote copies, remote signals or barrier semaphores. Data moves between devices by JAX's collectives and lax.ppermute only.
A program may use at most 128 MiB of HBM per device.

```python
import math
import jax
import jax.numpy as jnp
from jax import lax

D = 2048
Q_HEADS = 32
KV_HEADS = 8
HEAD_DIM = 64
LIVE_VOCAB = 49155
TOK_DEV = 192
VOCAB = 49408
TOKENS = 6144
SHORTS = 24
DOCS = 26


def query_weight(key):
    return jax.random.normal(jax.random.fold_in(key, 211), (D, Q_HEADS * HEAD_DIM), jnp.float32) / math.sqrt(D)


def picked_columns(key):
    segment = LIVE_VOCAB // 6
    offsets = jax.random.randint(jax.random.fold_in(key, 231), (6,), 0, segment)
    return (jnp.arange(6, dtype=jnp.int32) * segment + offsets).astype(jnp.int32)


def vocab_tables(key):
    banned = jax.random.randint(jax.random.fold_in(key, 241), (VOCAB,), 0, 50) == 0
    vocab_index = jnp.arange(VOCAB, dtype=jnp.int32)
    live_table = ((vocab_index < LIVE_VOCAB) & jnp.logical_not(banned)).astype(jnp.int32)
    id_table = jax.random.randint(jax.random.fold_in(key, 242), (TOKENS,), 0, LIVE_VOCAB).astype(jnp.int32)
    spot_pos = jax.random.randint(jax.random.fold_in(key, 243), (), 0, TOKENS)
    id_table = id_table.at[spot_pos].set(LIVE_VOCAB - 1)
    id_table = id_table.at[(spot_pos + 1) % TOKENS].set(0)
    live_table = live_table.at[id_table].set(1)
    live_table = live_table.at[picked_columns(key)].set(1)
    return (live_table, id_table)


def draw_hidden_states(key, part):
    noise_part = jax.random.normal(jax.random.fold_in(key, 201), (TOKENS, D), jnp.float32)
    values = noise_part
    return values.astype(jnp.bfloat16)


def draw_w_q(key, part):
    return query_weight(key).astype(jnp.bfloat16)


def draw_w_k(key, part):
    noise_part = jax.random.normal(jax.random.fold_in(key, 212), (D, KV_HEADS * HEAD_DIM), jnp.float32) / math.sqrt(D)
    values = noise_part
    return values.astype(jnp.bfloat16)


def draw_w_head(key, part):
    base_part = jax.random.normal(jax.random.fold_in(key, 221), (D, VOCAB), jnp.float32) * (24.0 / math.sqrt(D))
    return base_part.astype(jnp.bfloat16)


def draw_doc_lengths(key, part):
    short_len = jax.random.randint(jax.random.fold_in(key, 251), (SHORTS,), 1, 64).astype(jnp.int32)
    long_one = jnp.full((1,), TOKENS // 2, jnp.int32)
    long_two = jnp.full((1,), TOKENS - TOKENS // 2, jnp.int32) - jnp.sum(short_len)
    all_lengths = jnp.concatenate([long_one, long_two.astype(jnp.int32), short_len])
    shuffle = jax.random.permutation(jax.random.fold_in(key, 252), DOCS)
    return all_lengths[shuffle].astype(jnp.int32)


def draw_target_ids(key, part):
    return vocab_tables(key)[1]


def draw_vocab_mask(key, part):
    return vocab_tables(key)[0]


def block_scale(stream_key, shape, cuts, low, top_value):
    def one(dim, parts):
        draws = jax.random.uniform(jax.random.fold_in(jax.random.fold_in(stream_key, 6), dim), (parts,), jnp.float32, low / len(cuts), top_value / len(cuts))
        return jnp.repeat(jnp.exp(draws), shape[dim] // parts).reshape((-1,) + (1,) * (len(shape) - dim - 1))

    level = one(*cuts[0])
    for cut in cuts[1:]:
        level = level * one(*cut)
    return level


def centred(own_key, dims, deviation, bound, cuts=(), held_as=jnp.bfloat16):
    values = jax.random.normal(own_key, dims, jnp.float32) * deviation
    if len(cuts) > 0:
        values = block_scale(own_key, dims, cuts, -0.22, 0.18) * values
    return jnp.clip(values, min=-bound, max=bound).astype(held_as)


def setup_inputs(seed: int = 0) -> dict:
    seeds = jax.random.split(jax.random.key(seed), 12)
    return {
        "hidden_states": draw_hidden_states(jax.random.fold_in(seeds[11], 71), 0),
        "attn_gain": jnp.clip(1.0 + 0.1 * jax.random.normal(seeds[1], (D,), jnp.float32), 0.5, 1.5),
        "w_q": draw_w_q(jax.random.fold_in(seeds[11], 71), 0),
        "w_k": draw_w_k(jax.random.fold_in(seeds[11], 71), 0),
        "w_v": centred(seeds[4], (D, KV_HEADS * HEAD_DIM), D ** -0.5, 0.125, ((1, 8),)),
        "w_o": centred(seeds[5], (Q_HEADS * HEAD_DIM, D), (Q_HEADS * HEAD_DIM) ** -0.5, 0.125, ((0, 8),)),
        "final_gain": jnp.clip(1.0 + 0.1 * jax.random.normal(seeds[6], (D,), jnp.float32), 0.5, 1.5),
        "w_head": draw_w_head(jax.random.fold_in(seeds[11], 71), 0),
        "doc_lengths": draw_doc_lengths(jax.random.fold_in(seeds[11], 71), 0),
        "target_ids": draw_target_ids(jax.random.fold_in(seeds[11], 71), 0),
        "vocab_mask": draw_vocab_mask(jax.random.fold_in(seeds[11], 71), 0),
    }


ROPE_THETA = 10000000.0
NORM_EPS = 1e-05
NEG_FILL = -1e+30
ATTN_SCALE = 0.015625
RESID_SCALE = 5.0
LOGIT_SCALE = 0.125

def rms_norm(values, gain_vec):
    return values * lax.rsqrt(lax.optimization_barrier(jnp.mean(values * values, axis=-1, keepdims=True)) + NORM_EPS) * gain_vec

def rotate(values, positions):
    half_dim = values.shape[-1] // 2
    inverse = jnp.exp(jnp.arange(half_dim, dtype=jnp.float32) * (-2.0 * math.log(ROPE_THETA) / values.shape[-1]))
    angles = positions.astype(jnp.float32)[:, None] * inverse[None, :]
    cos_val = jnp.cos(angles)[:, None, :]
    sine_val = jnp.sin(angles)[:, None, :]
    lower_half = values[..., :half_dim]
    upper_half = values[..., half_dim:]
    return jnp.concatenate([lower_half * cos_val - upper_half * sine_val, upper_half * cos_val + lower_half * sine_val], axis=-1)

def reference(hidden_states, attn_gain, w_q, w_k, w_v, w_o, final_gain, w_head, doc_lengths, target_ids, vocab_mask):
    stream = hidden_states.astype(jnp.float32)
    normed_in = rms_norm(stream, attn_gain).astype(jnp.bfloat16)
    queries = jnp.dot(normed_in, w_q, preferred_element_type=jnp.float32)
    key_proj = jnp.dot(normed_in, w_k, preferred_element_type=jnp.float32)
    value_proj = jnp.dot(normed_in, w_v, preferred_element_type=jnp.float32)
    doc_ends = jnp.cumsum(doc_lengths).astype(jnp.int32)
    doc_starts = (doc_ends - doc_lengths).astype(jnp.int32)
    token_pos = jnp.arange(TOKENS, dtype=jnp.int32)
    doc_start = lax.optimization_barrier(jnp.max(jnp.where(doc_starts[None, :] <= token_pos[:, None], doc_starts[None, :], 0), axis=1)).astype(jnp.int32)
    positions = token_pos - doc_start
    group_size = Q_HEADS // KV_HEADS
    rotated_q = rotate(queries.reshape(TOKENS, Q_HEADS, HEAD_DIM), positions).astype(jnp.bfloat16)
    rotated_q = rotated_q.reshape(TOKENS, KV_HEADS, group_size, HEAD_DIM)
    rotated_k = rotate(key_proj.reshape(TOKENS, KV_HEADS, HEAD_DIM), positions).astype(jnp.bfloat16)
    value_rows = value_proj.astype(jnp.bfloat16).reshape(TOKENS, KV_HEADS, HEAD_DIM)
    keys_f32 = rotated_k.astype(jnp.float32)
    values_f32 = value_rows.astype(jnp.float32)

    def attend(block_idx):
        row_first = (block_idx * TOK_DEV).astype(jnp.int32)
        q_block = lax.dynamic_slice_in_dim(rotated_q, row_first, TOK_DEV, 0).astype(jnp.float32)
        query_pos = row_first + jnp.arange(TOK_DEV, dtype=jnp.int32)
        query_start = lax.dynamic_slice_in_dim(doc_start, row_first, TOK_DEV, 0)
        scores = jnp.einsum('tkgd,skd->kgts', q_block, keys_f32) * ATTN_SCALE
        allowed = (token_pos[None, :] >= query_start[:, None]) & (token_pos[None, :] <= query_pos[:, None])
        scores = jnp.where(allowed, scores, NEG_FILL)
        top_score = lax.optimization_barrier(jnp.max(scores, axis=-1, keepdims=True))
        weights = jnp.where(allowed, jnp.exp(scores - top_score), 0.0)
        totals = lax.optimization_barrier(jnp.sum(weights, axis=-1))
        rounded = lax.optimization_barrier(weights.astype(jnp.bfloat16)).astype(jnp.float32)
        context = jnp.einsum('kgts,skd->kgtd', rounded, values_f32) / totals[..., None]
        return context.transpose(2, 0, 1, 3).reshape(TOK_DEV, Q_HEADS * HEAD_DIM).astype(jnp.bfloat16)
    context_all = lax.map(attend, jnp.arange(TOKENS // TOK_DEV, dtype=jnp.int32)).reshape(TOKENS, Q_HEADS * HEAD_DIM)
    attn_out = jnp.dot(context_all, w_o, preferred_element_type=jnp.float32)
    final_in = rms_norm(stream + RESID_SCALE * attn_out, final_gain).astype(jnp.bfloat16)
    live_mask = vocab_mask == 1

    def score(block_idx):
        row_first = (block_idx * TOK_DEV).astype(jnp.int32)
        rows = lax.dynamic_slice_in_dim(final_in, row_first, TOK_DEV, 0)
        row_ids = lax.dynamic_slice_in_dim(target_ids, row_first, TOK_DEV, 0)
        logits = jnp.dot(rows, w_head, preferred_element_type=jnp.float32) * LOGIT_SCALE
        masked = jnp.where(live_mask[None, :], logits, NEG_FILL)
        top_score = lax.optimization_barrier(jnp.max(masked, axis=1, keepdims=True))
        expw = jnp.where(live_mask[None, :], jnp.exp(masked - top_score), 0.0)
        totals = lax.optimization_barrier(jnp.sum(expw, axis=1, keepdims=True))
        log_total = top_score + jnp.log(totals)
        probs = expw / totals
        entropy = log_total[:, 0] - lax.optimization_barrier(jnp.sum(probs * jnp.where(live_mask[None, :], logits, 0.0), axis=1))
        target = jnp.take_along_axis(logits, row_ids[:, None].astype(jnp.int32), axis=1)[:, 0]
        return (target - log_total[:, 0], entropy)
    log_probs, entropies = lax.map(score, jnp.arange(TOKENS // TOK_DEV, dtype=jnp.int32))
    return (log_probs.reshape(TOKENS), entropies.reshape(TOKENS))
```

```python
import math

import jax
import jax.numpy as jnp
from jax import lax
from jax.sharding import Mesh, PartitionSpec as P

HEAD_DIM = 64


ROPE_THETA = 10000000.0
NORM_EPS = 1e-05
NEG_FILL = -1e30
ATTN_SCALE = 0.015625
RESID_SCALE = 5.0
LOGIT_SCALE = 0.125


def rms_norm(values, gain_vec):
    return (
        values * lax.rsqrt(jnp.mean(values * values, axis=-1, keepdims=True) + NORM_EPS) * gain_vec
    )


def rotate(values, positions):
    half_dim = values.shape[-1] // 2
    inverse = jnp.exp(
        jnp.arange(half_dim, dtype=jnp.float32) * (-2.0 * math.log(ROPE_THETA) / values.shape[-1])
    )
    angles = positions.astype(jnp.float32)[:, None] * inverse[None, :]
    cos_val = jnp.cos(angles)[:, None, :]
    sine_val = jnp.sin(angles)[:, None, :]
    lower_half = values[..., :half_dim]
    upper_half = values[..., half_dim:]
    return jnp.concatenate(
        [
            lower_half * cos_val - upper_half * sine_val,
            upper_half * cos_val + lower_half * sine_val,
        ],
        axis=-1,
    )


def local(
    hidden_states,
    attn_gain,
    w_q,
    w_k,
    w_v,
    w_o,
    final_gain,
    w_head,
    doc_lengths,
    target_ids,
    vocab_mask,
):
    tok_rows = hidden_states.shape[0]
    seq_index = lax.axis_index(("z", "y"))
    kv_local = w_k.shape[1] // HEAD_DIM
    q_local = w_q.shape[1] // HEAD_DIM
    group_size = q_local // kv_local
    key_width = kv_local * HEAD_DIM
    stream = hidden_states.astype(jnp.float32)
    normed_in = rms_norm(stream, attn_gain).astype(jnp.bfloat16)
    queries = jnp.dot(normed_in, w_q, preferred_element_type=jnp.float32)
    key_proj = jnp.dot(normed_in, w_k, preferred_element_type=jnp.float32)
    value_proj = jnp.dot(normed_in, w_v, preferred_element_type=jnp.float32)
    token_pos = seq_index * tok_rows + jnp.arange(tok_rows, dtype=jnp.int32)
    doc_ends = jnp.cumsum(doc_lengths)
    doc_starts = doc_ends - doc_lengths
    doc_start = jnp.max(
        jnp.where(doc_starts[None, :] <= token_pos[:, None], doc_starts[None, :], 0), axis=1
    )
    positions = token_pos - doc_start
    rotated_q = rotate(queries.reshape(tok_rows, q_local, HEAD_DIM), positions).astype(jnp.bfloat16)
    rotated_q = rotated_q.reshape(tok_rows, kv_local, group_size, HEAD_DIM)
    rotated_k = rotate(key_proj.reshape(tok_rows, kv_local, HEAD_DIM), positions).astype(
        jnp.bfloat16
    )
    packed = jnp.concatenate(
        [rotated_k.reshape(tok_rows, key_width), value_proj.astype(jnp.bfloat16)], axis=1
    )
    earliest = doc_start[0]
    latest = token_pos[tok_rows - 1]
    initial = (
        jnp.full((kv_local, group_size, tok_rows), NEG_FILL, jnp.float32),
        jnp.zeros((kv_local, group_size, tok_rows), jnp.float32),
        jnp.zeros((kv_local, group_size, tok_rows, HEAD_DIM), jnp.float32),
    )
    shard_rows = lax.all_gather(packed, ("z", "y"), axis=0, tiled=True)
    offset = jnp.int32(0)
    row_count = shard_rows.shape[0]
    key_pos = jnp.arange(row_count, dtype=jnp.int32)

    def update(current):
        top_score, totals, context_sum = current
        key_rows = shard_rows[:, :key_width].reshape(row_count, kv_local, HEAD_DIM)
        value_rows = shard_rows[:, key_width:].reshape(row_count, kv_local, HEAD_DIM)
        scores = (
            jnp.einsum("tkgd,skd->kgts", rotated_q, key_rows, preferred_element_type=jnp.float32)
            * ATTN_SCALE
        )
        allowed = (key_pos[None, :] >= doc_start[:, None]) & (
            key_pos[None, :] <= token_pos[:, None]
        )
        scores = jnp.where(allowed, scores, NEG_FILL)
        new_top = jnp.maximum(top_score, jnp.max(scores, axis=-1))
        weights = jnp.where(allowed, jnp.exp(scores - new_top[..., None]), 0.0)
        rescale = jnp.exp(top_score - new_top)
        totals = jnp.sum(weights, axis=-1)
        context_sum = jnp.einsum(
            "kgts,skd->kgtd",
            weights.astype(jnp.bfloat16),
            value_rows,
            preferred_element_type=jnp.float32,
        )
        return (new_top, totals, context_sum)

    skip_piece = (offset + row_count <= earliest) | (offset > latest)
    top_score, totals, context_sum = lax.cond(skip_piece, lambda current: current, update, initial)
    context = (
        (context_sum / totals[..., None])
        .transpose(2, 0, 1, 3)
        .reshape(tok_rows, q_local * HEAD_DIM)
        .astype(jnp.bfloat16)
    )
    vocab_local = w_head.shape[1]
    y_count = lax.psum(1, "y")
    z_count = lax.psum(1, "z")
    z_index = lax.axis_index("z")
    y_index = lax.axis_index("y")
    kv_index = lax.axis_index("kv")
    attn_out = lax.psum(jnp.dot(context, w_o, preferred_element_type=jnp.float32), "kv")
    final_in = rms_norm(stream + RESID_SCALE * attn_out, final_gain).astype(jnp.bfloat16)
    head_rows = lax.all_gather(final_in, "y", axis=0, tiled=True)
    group_rows = head_rows.shape[0]
    head_cols = lax.all_gather(w_head, "z", axis=1, tiled=True)
    mask_cols = lax.all_gather(vocab_mask, "z", axis=0, tiled=True)
    live_mask = mask_cols == 1
    shard_ids = kv_index * (z_count * y_count) + jnp.arange(z_count, dtype=jnp.int32) * y_count + y_index
    columns = (shard_ids[:, None] * vocab_local + jnp.arange(vocab_local, dtype=jnp.int32)[None, :]).reshape(-1)
    row_ids = lax.dynamic_slice_in_dim(target_ids, z_index * group_rows, group_rows, 0)
    logits = jnp.dot(head_rows, head_cols, preferred_element_type=jnp.float32) * LOGIT_SCALE
    masked = jnp.where(live_mask[None, :], logits, NEG_FILL)
    top_row = jnp.max(masked, axis=1)
    shifted = jnp.where(live_mask[None, :], masked - top_row[:, None], 0.0)
    expw = jnp.where(live_mask[None, :], jnp.exp(shifted), 0.0)
    target = jnp.sum(jnp.where(row_ids[:, None] == columns[None, :], logits, 0.0), axis=1)
    row_stats = jnp.stack([top_row, jnp.sum(expw, axis=1), jnp.sum(expw * shifted, axis=1), target])
    top_all = lax.pmax(row_stats[0], ("kv", "y"))
    rescale = jnp.exp(row_stats[0] - top_all)
    total_all, spread_all, target_all = lax.psum(
        (
            row_stats[1] * rescale,
            rescale * (row_stats[2] + (row_stats[0] - top_all) * row_stats[1]),
            row_stats[3],
        ),
        ("kv", "y"),
    )
    log_prob = target_all - top_all - jnp.log(total_all)
    entropy = jnp.log(total_all) - spread_all / total_all
    log_probs = lax.dynamic_slice_in_dim(log_prob, y_index * tok_rows, tok_rows, 0)
    entropies = lax.dynamic_slice_in_dim(entropy, y_index * tok_rows, tok_rows, 0)
    return (log_probs, entropies)


def solution(mesh):
    kv_size, seq_size = mesh.devices.shape
    z_size = mesh.shape["seq"] // 4 if mesh.shape["seq"] % 4 == 0 else mesh.shape["seq"]
    y_size = seq_size // z_size
    split_mesh = Mesh(mesh.devices.reshape(kv_size, z_size, y_size), ("kv", "z", "y"))
    seq = ("z", "y")
    in_specs = (
        P(seq, None),
        P(),
        P(None, "kv"),
        P(None, "kv"),
        P(None, "kv"),
        P("kv", None),
        P(),
        P(None, ("kv",) + seq),
        P(),
        P(),
        P(("kv",) + seq),
    )
    out_specs = (P(seq), P(seq))
    return jax.shard_map(local, mesh=split_mesh, in_specs=in_specs, out_specs=out_specs, check_vma=False)
```

```python
import math

import jax
import jax.numpy as jnp
from jax import lax
from jax.sharding import Mesh, PartitionSpec as P

HEAD_DIM = 64


ROPE_THETA = 10000000.0
NORM_EPS = 1e-05
NEG_FILL = -1e30
ATTN_SCALE = 0.015625
RESID_SCALE = 5.0
LOGIT_SCALE = 0.125


def rms_norm(values, gain_vec):
    return (
        values * lax.rsqrt(jnp.mean(values * values, axis=-1, keepdims=True) + NORM_EPS) * gain_vec
    )


def rotate(values, positions):
    half_dim = values.shape[-1] // 2
    inverse = jnp.exp(
        jnp.arange(half_dim, dtype=jnp.float32) * (-2.0 * math.log(ROPE_THETA) / values.shape[-1])
    )
    angles = positions.astype(jnp.float32)[:, None] * inverse[None, :]
    cos_val = jnp.cos(angles)[:, None, :]
    sine_val = jnp.sin(angles)[:, None, :]
    lower_half = values[..., :half_dim]
    upper_half = values[..., half_dim:]
    return jnp.concatenate(
        [
            lower_half * cos_val - upper_half * sine_val,
            upper_half * cos_val + lower_half * sine_val,
        ],
        axis=-1,
    )


def merge_stats(mine, other, mine_first):
    first = jnp.where(mine_first, mine, other)
    second = jnp.where(mine_first, other, mine)
    top = jnp.maximum(first[0], second[0])
    gap_a = first[0] - top
    gap_b = second[0] - top
    scale_a = jnp.exp(gap_a)
    scale_b = jnp.exp(gap_b)
    total = first[1] * scale_a + second[1] * scale_b
    spread = scale_a * (first[2] + gap_a * first[1]) + scale_b * (second[2] + gap_b * second[1])
    target = first[3] + second[3]
    return jnp.stack([top, total, spread, target])


def local(
    hidden_states,
    attn_gain,
    w_q,
    w_k,
    w_v,
    w_o,
    final_gain,
    w_head,
    doc_lengths,
    target_ids,
    vocab_mask,
):
    tok_rows = hidden_states.shape[0]
    seq_index = lax.axis_index(("z", "y"))
    kv_local = w_k.shape[1] // HEAD_DIM
    q_local = w_q.shape[1] // HEAD_DIM
    group_size = q_local // kv_local
    key_width = kv_local * HEAD_DIM
    stream = hidden_states.astype(jnp.float32)
    normed_in = rms_norm(stream, attn_gain).astype(jnp.bfloat16)
    queries = jnp.dot(normed_in, w_q, preferred_element_type=jnp.float32)
    key_proj = jnp.dot(normed_in, w_k, preferred_element_type=jnp.float32)
    value_proj = jnp.dot(normed_in, w_v, preferred_element_type=jnp.float32)
    token_pos = seq_index * tok_rows + jnp.arange(tok_rows, dtype=jnp.int32)
    doc_ends = jnp.cumsum(doc_lengths)
    doc_starts = doc_ends - doc_lengths
    doc_start = jnp.max(
        jnp.where(doc_starts[None, :] <= token_pos[:, None], doc_starts[None, :], 0), axis=1
    )
    positions = token_pos - doc_start
    rotated_q = rotate(queries.reshape(tok_rows, q_local, HEAD_DIM), positions).astype(jnp.bfloat16)
    rotated_q = rotated_q.reshape(tok_rows, kv_local, group_size, HEAD_DIM)
    rotated_k = rotate(key_proj.reshape(tok_rows, kv_local, HEAD_DIM), positions).astype(
        jnp.bfloat16
    )
    packed = jnp.concatenate(
        [rotated_k.reshape(tok_rows, key_width), value_proj.astype(jnp.bfloat16)], axis=1
    )
    earliest = doc_start[0]
    latest = token_pos[tok_rows - 1]
    initial = (
        jnp.full((kv_local, group_size, tok_rows), NEG_FILL, jnp.float32),
        jnp.zeros((kv_local, group_size, tok_rows), jnp.float32),
        jnp.zeros((kv_local, group_size, tok_rows, HEAD_DIM), jnp.float32),
    )
    shard_rows = lax.all_gather(packed, ("z", "y"), axis=0, tiled=True)
    offset = jnp.int32(0)
    row_count = shard_rows.shape[0]
    key_pos = jnp.arange(row_count, dtype=jnp.int32)

    def update(current):
        top_score, totals, context_sum = current
        key_rows = shard_rows[:, :key_width].reshape(row_count, kv_local, HEAD_DIM)
        value_rows = shard_rows[:, key_width:].reshape(row_count, kv_local, HEAD_DIM)
        scores = (
            jnp.einsum("tkgd,skd->kgts", rotated_q, key_rows, preferred_element_type=jnp.float32)
            * ATTN_SCALE
        )
        allowed = (key_pos[None, :] >= doc_start[:, None]) & (
            key_pos[None, :] <= token_pos[:, None]
        )
        scores = jnp.where(allowed, scores, NEG_FILL)
        new_top = jnp.maximum(top_score, jnp.max(scores, axis=-1))
        weights = jnp.where(allowed, jnp.exp(scores - new_top[..., None]), 0.0)
        rescale = jnp.exp(top_score - new_top)
        totals = jnp.sum(weights, axis=-1)
        context_sum = jnp.einsum(
            "kgts,skd->kgtd",
            weights.astype(jnp.bfloat16),
            value_rows,
            preferred_element_type=jnp.float32,
        )
        return (new_top, totals, context_sum)

    skip_piece = (offset + row_count <= earliest) | (offset > latest)
    top_score, totals, context_sum = lax.cond(skip_piece, lambda current: current, update, initial)
    context = (
        (context_sum / totals[..., None])
        .transpose(2, 0, 1, 3)
        .reshape(tok_rows, q_local * HEAD_DIM)
        .astype(jnp.bfloat16)
    )
    vocab_local = w_head.shape[1]
    y_count = lax.psum(1, "y")
    z_count = lax.psum(1, "z")
    z_index = lax.axis_index("z")
    y_index = lax.axis_index("y")
    kv_index = lax.axis_index("kv")
    attn_out = lax.psum(jnp.dot(context, w_o, preferred_element_type=jnp.float32), "kv")
    final_in = rms_norm(stream + RESID_SCALE * attn_out, final_gain).astype(jnp.bfloat16)
    head_rows = lax.all_gather(final_in, "y", axis=0, tiled=True)
    group_rows = head_rows.shape[0]
    head_cols = lax.all_gather(w_head, "z", axis=1, tiled=True)
    mask_cols = lax.all_gather(vocab_mask.astype(jnp.float32), "z", axis=0, tiled=True)
    live_mask = mask_cols == 1.0
    shard_ids = kv_index * (z_count * y_count) + jnp.arange(z_count, dtype=jnp.int32) * y_count + y_index
    columns = (shard_ids[:, None] * vocab_local + jnp.arange(vocab_local, dtype=jnp.int32)[None, :]).reshape(-1)
    row_ids = lax.dynamic_slice_in_dim(target_ids, z_index * group_rows, group_rows, 0)
    logits = jnp.dot(head_rows, head_cols, preferred_element_type=jnp.float32) * LOGIT_SCALE
    masked = jnp.where(live_mask[None, :], logits, NEG_FILL)
    top_row = jnp.max(masked, axis=1)
    shifted = jnp.where(live_mask[None, :], masked - top_row[:, None], 0.0)
    expw = jnp.where(live_mask[None, :], jnp.exp(shifted), 0.0)
    target = jnp.sum(jnp.where(row_ids[:, None] == columns[None, :], logits, 0.0), axis=1)
    row_stats = jnp.stack(
        [top_row, jnp.sum(expw, axis=1), jnp.sum(expw * shifted, axis=1), target]
    ).reshape(4, y_count, tok_rows)
    half = y_count // 2
    my_half = y_index // half
    keep = lax.dynamic_slice_in_dim(row_stats, my_half * half, half, 1)
    send = lax.dynamic_slice_in_dim(row_stats, (1 - my_half) * half, half, 1)
    got = lax.ppermute(send, "y", [(p, p ^ half) for p in range(y_count)])
    merged = merge_stats(keep, got, my_half == 0)
    width = half
    while width > 1:
        width //= 2
        my_part = (y_index // width) % 2
        keep = lax.dynamic_slice_in_dim(merged, my_part * width, width, 1)
        send = lax.dynamic_slice_in_dim(merged, (1 - my_part) * width, width, 1)
        got = lax.ppermute(send, "y", [(p, p ^ width) for p in range(y_count)])
        merged = merge_stats(keep, got, my_part == 0)
    merged = merged[:, 0]
    kv_count = lax.psum(1, "kv")
    step = 1
    while step < kv_count:
        got = lax.ppermute(merged, "kv", [(p, p ^ step) for p in range(kv_count)])
        merged = merge_stats(merged, got, (kv_index // step) % 2 == 0)
        step *= 2
    top_all, total_all, spread_all, target_all = merged[0], merged[1], merged[2], merged[3]
    log_probs = target_all - top_all - jnp.log(total_all)
    entropies = jnp.log(total_all) - spread_all / total_all
    return (log_probs, entropies)


def solution(mesh):
    kv_size, seq_size = mesh.devices.shape
    z_size = mesh.shape["seq"] // 4 if mesh.shape["seq"] % 4 == 0 else mesh.shape["seq"]
    y_size = seq_size // z_size
    split_mesh = Mesh(mesh.devices.reshape(kv_size, z_size, y_size), ("kv", "z", "y"))
    seq = ("z", "y")
    in_specs = (
        P(seq, None),
        P(),
        P(None, "kv"),
        P(None, "kv"),
        P(None, "kv"),
        P("kv", None),
        P(),
        P(None, ("kv",) + seq),
        P(),
        P(),
        P(("kv",) + seq),
    )
    out_specs = (P(seq), P(seq))
    return jax.shard_map(local, mesh=split_mesh, in_specs=in_specs, out_specs=out_specs, check_vma=False)
```

```python
import math

import jax
import jax.numpy as jnp
from jax import lax
from jax.sharding import Mesh, PartitionSpec as P

HEAD_DIM = 64


ROPE_THETA = 10000000.0
NORM_EPS = 1e-05
NEG_FILL = -1e30
ATTN_SCALE = 0.015625
RESID_SCALE = 5.0
LOGIT_SCALE = 0.125


def rms_norm(values, gain_vec):
    return (
        values * lax.rsqrt(jnp.mean(values * values, axis=-1, keepdims=True) + NORM_EPS) * gain_vec
    )


def rotate(values, positions):
    half_dim = values.shape[-1] // 2
    inverse = jnp.exp(
        jnp.arange(half_dim, dtype=jnp.float32) * (-2.0 * math.log(ROPE_THETA) / values.shape[-1])
    )
    angles = positions.astype(jnp.float32)[:, None] * inverse[None, :]
    cos_val = jnp.cos(angles)[:, None, :]
    sine_val = jnp.sin(angles)[:, None, :]
    lower_half = values[..., :half_dim]
    upper_half = values[..., half_dim:]
    return jnp.concatenate(
        [
            lower_half * cos_val - upper_half * sine_val,
            upper_half * cos_val + lower_half * sine_val,
        ],
        axis=-1,
    )


def merge_stats(mine, other, mine_first):
    first = jnp.where(mine_first, mine, other)
    second = jnp.where(mine_first, other, mine)
    top = jnp.maximum(first[0], second[0])
    gap_a = first[0] - top
    gap_b = second[0] - top
    scale_a = jnp.exp(gap_a)
    scale_b = jnp.exp(gap_b)
    total = first[1] * scale_a + second[1] * scale_b
    spread = scale_a * (first[2] + gap_a * first[1]) + scale_b * (second[2] + gap_b * second[1])
    target = first[3] + second[3]
    return jnp.stack([top, total, spread, target])


def local(
    hidden_states,
    attn_gain,
    w_q,
    w_k,
    w_v,
    w_o,
    final_gain,
    w_head,
    doc_lengths,
    target_ids,
    vocab_mask,
):
    tok_rows = hidden_states.shape[0]
    seq_index = lax.axis_index(("z", "y"))
    kv_local = w_k.shape[1] // HEAD_DIM
    q_local = w_q.shape[1] // HEAD_DIM
    group_size = q_local // kv_local
    key_width = kv_local * HEAD_DIM
    stream = hidden_states.astype(jnp.float32)
    normed_in = rms_norm(stream, attn_gain).astype(jnp.bfloat16)
    queries = jnp.dot(normed_in, w_q, preferred_element_type=jnp.float32)
    key_proj = jnp.dot(normed_in, w_k, preferred_element_type=jnp.float32)
    value_proj = jnp.dot(normed_in, w_v, preferred_element_type=jnp.float32)
    token_pos = seq_index * tok_rows + jnp.arange(tok_rows, dtype=jnp.int32)
    doc_ends = jnp.cumsum(doc_lengths)
    doc_starts = doc_ends - doc_lengths
    doc_start = jnp.max(
        jnp.where(doc_starts[None, :] <= token_pos[:, None], doc_starts[None, :], 0), axis=1
    )
    positions = token_pos - doc_start
    rotated_q = rotate(queries.reshape(tok_rows, q_local, HEAD_DIM), positions).astype(jnp.bfloat16)
    rotated_q = rotated_q.reshape(tok_rows, kv_local, group_size, HEAD_DIM)
    rotated_k = rotate(key_proj.reshape(tok_rows, kv_local, HEAD_DIM), positions).astype(
        jnp.bfloat16
    )
    packed = jnp.concatenate(
        [rotated_k.reshape(tok_rows, key_width), value_proj.astype(jnp.bfloat16)], axis=1
    )
    earliest = doc_start[0]
    latest = token_pos[tok_rows - 1]
    initial = (
        jnp.full((kv_local, group_size, tok_rows), NEG_FILL, jnp.float32),
        jnp.zeros((kv_local, group_size, tok_rows), jnp.float32),
        jnp.zeros((kv_local, group_size, tok_rows, HEAD_DIM), jnp.float32),
    )
    shard_rows = lax.all_gather(packed, ("z", "y"), axis=0, tiled=True)
    head_pad = jnp.zeros((16 - 1, w_head.shape[1]), w_head.dtype)
    head_ext = jnp.concatenate([w_head, vocab_mask.astype(w_head.dtype)[None, :], head_pad], axis=0)
    head_ext = lax.all_gather(head_ext, "z", axis=1, tiled=True)
    shard_rows, head_ext = lax.optimization_barrier((shard_rows, head_ext))
    head_cols = head_ext[: w_head.shape[0]]
    mask_cols = head_ext[w_head.shape[0]]
    offset = jnp.int32(0)
    row_count = shard_rows.shape[0]
    key_pos = jnp.arange(row_count, dtype=jnp.int32)

    def update(current):
        top_score, totals, context_sum = current
        key_rows = shard_rows[:, :key_width].reshape(row_count, kv_local, HEAD_DIM)
        value_rows = shard_rows[:, key_width:].reshape(row_count, kv_local, HEAD_DIM)
        scores = (
            jnp.einsum("tkgd,skd->kgts", rotated_q, key_rows, preferred_element_type=jnp.float32)
            * ATTN_SCALE
        )
        allowed = (key_pos[None, :] >= doc_start[:, None]) & (
            key_pos[None, :] <= token_pos[:, None]
        )
        scores = jnp.where(allowed, scores, NEG_FILL)
        new_top = jnp.maximum(top_score, jnp.max(scores, axis=-1))
        weights = jnp.where(allowed, jnp.exp(scores - new_top[..., None]), 0.0)
        rescale = jnp.exp(top_score - new_top)
        totals = jnp.sum(weights, axis=-1)
        context_sum = jnp.einsum(
            "kgts,skd->kgtd",
            weights.astype(jnp.bfloat16),
            value_rows,
            preferred_element_type=jnp.float32,
        )
        return (new_top, totals, context_sum)

    skip_piece = (offset + row_count <= earliest) | (offset > latest)
    top_score, totals, context_sum = lax.cond(skip_piece, lambda current: current, update, initial)
    context = (
        (context_sum / totals[..., None])
        .transpose(2, 0, 1, 3)
        .reshape(tok_rows, q_local * HEAD_DIM)
        .astype(jnp.bfloat16)
    )
    vocab_local = w_head.shape[1]
    y_count = lax.psum(1, "y")
    z_count = lax.psum(1, "z")
    z_index = lax.axis_index("z")
    y_index = lax.axis_index("y")
    kv_index = lax.axis_index("kv")
    attn_out = lax.psum(jnp.dot(context, w_o, preferred_element_type=jnp.float32), "kv")
    final_in = rms_norm(stream + RESID_SCALE * attn_out, final_gain).astype(jnp.bfloat16)
    head_rows = lax.all_gather(final_in, "y", axis=0, tiled=True)
    group_rows = head_rows.shape[0]
    live_mask = mask_cols == 1.0
    shard_ids = kv_index * (z_count * y_count) + jnp.arange(z_count, dtype=jnp.int32) * y_count + y_index
    columns = (shard_ids[:, None] * vocab_local + jnp.arange(vocab_local, dtype=jnp.int32)[None, :]).reshape(-1)
    row_ids = lax.dynamic_slice_in_dim(target_ids, z_index * group_rows, group_rows, 0)
    logits = jnp.dot(head_rows, head_cols, preferred_element_type=jnp.float32) * LOGIT_SCALE
    masked = jnp.where(live_mask[None, :], logits, NEG_FILL)
    top_row = jnp.max(masked, axis=1)
    shifted = jnp.where(live_mask[None, :], masked - top_row[:, None], 0.0)
    expw = jnp.where(live_mask[None, :], jnp.exp(shifted), 0.0)
    target = jnp.sum(jnp.where(row_ids[:, None] == columns[None, :], logits, 0.0), axis=1)
    row_stats = jnp.stack(
        [top_row, jnp.sum(expw, axis=1), jnp.sum(expw * shifted, axis=1), target]
    ).reshape(4, y_count, tok_rows)
    half = y_count // 2
    my_half = y_index // half
    keep = lax.dynamic_slice_in_dim(row_stats, my_half * half, half, 1)
    send = lax.dynamic_slice_in_dim(row_stats, (1 - my_half) * half, half, 1)
    got = lax.ppermute(send, "y", [(p, p ^ half) for p in range(y_count)])
    merged = merge_stats(keep, got, my_half == 0)
    width = half
    while width > 1:
        width //= 2
        my_part = (y_index // width) % 2
        keep = lax.dynamic_slice_in_dim(merged, my_part * width, width, 1)
        send = lax.dynamic_slice_in_dim(merged, (1 - my_part) * width, width, 1)
        got = lax.ppermute(send, "y", [(p, p ^ width) for p in range(y_count)])
        merged = merge_stats(keep, got, my_part == 0)
    merged = merged[:, 0]
    kv_count = lax.psum(1, "kv")
    step = 1
    while step < kv_count:
        got = lax.ppermute(merged, "kv", [(p, p ^ step) for p in range(kv_count)])
        merged = merge_stats(merged, got, (kv_index // step) % 2 == 0)
        step *= 2
    top_all, total_all, spread_all, target_all = merged[0], merged[1], merged[2], merged[3]
    log_probs = target_all - top_all - jnp.log(total_all)
    entropies = jnp.log(total_all) - spread_all / total_all
    return (log_probs, entropies)


def solution(mesh):
    kv_size, seq_size = mesh.devices.shape
    z_size = mesh.shape["seq"] // 4 if mesh.shape["seq"] % 4 == 0 else mesh.shape["seq"]
    y_size = seq_size // z_size
    split_mesh = Mesh(mesh.devices.reshape(kv_size, z_size, y_size), ("kv", "z", "y"))
    seq = ("z", "y")
    in_specs = (
        P(seq, None),
        P(),
        P(None, "kv"),
        P(None, "kv"),
        P(None, "kv"),
        P("kv", None),
        P(),
        P(None, ("kv",) + seq),
        P(),
        P(),
        P(("kv",) + seq),
    )
    out_specs = (P(seq), P(seq))
    return jax.shard_map(local, mesh=split_mesh, in_specs=in_specs, out_specs=out_specs, check_vma=False)
```

```python
import math

import jax
import jax.numpy as jnp
from jax import lax
from jax.sharding import Mesh, PartitionSpec as P

HEAD_DIM = 64


ROPE_THETA = 10000000.0
NORM_EPS = 1e-05
NEG_FILL = -1e30
ATTN_SCALE = 0.015625
RESID_SCALE = 5.0
LOGIT_SCALE = 0.125


def rms_norm(values, gain_vec):
    return (
        values * lax.rsqrt(jnp.mean(values * values, axis=-1, keepdims=True) + NORM_EPS) * gain_vec
    )


def rotate(values, positions):
    half_dim = values.shape[-1] // 2
    inverse = jnp.exp(
        jnp.arange(half_dim, dtype=jnp.float32) * (-2.0 * math.log(ROPE_THETA) / values.shape[-1])
    )
    angles = positions.astype(jnp.float32)[:, None] * inverse[None, :]
    cos_val = jnp.cos(angles)[:, None, :]
    sine_val = jnp.sin(angles)[:, None, :]
    lower_half = values[..., :half_dim]
    upper_half = values[..., half_dim:]
    return jnp.concatenate(
        [
            lower_half * cos_val - upper_half * sine_val,
            upper_half * cos_val + lower_half * sine_val,
        ],
        axis=-1,
    )


def merge_stats(mine, other, mine_first):
    first = jnp.where(mine_first, mine, other)
    second = jnp.where(mine_first, other, mine)
    top = jnp.maximum(first[0], second[0])
    gap_a = first[0] - top
    gap_b = second[0] - top
    scale_a = jnp.exp(gap_a)
    scale_b = jnp.exp(gap_b)
    total = first[1] * scale_a + second[1] * scale_b
    spread = scale_a * (first[2] + gap_a * first[1]) + scale_b * (second[2] + gap_b * second[1])
    target = first[3] + second[3]
    return jnp.stack([top, total, spread, target])


def local(
    hidden_states,
    attn_gain,
    w_q,
    w_k,
    w_v,
    w_o,
    final_gain,
    w_head,
    doc_lengths,
    target_ids,
    vocab_mask,
):
    tok_rows = hidden_states.shape[0]
    seq_index = lax.axis_index(("z", "y"))
    kv_local = w_k.shape[1] // HEAD_DIM
    q_local = w_q.shape[1] // HEAD_DIM
    group_size = q_local // kv_local
    key_width = kv_local * HEAD_DIM
    stream = hidden_states.astype(jnp.float32)
    normed_in = rms_norm(stream, attn_gain).astype(jnp.bfloat16)
    queries = jnp.dot(normed_in, w_q, preferred_element_type=jnp.float32)
    key_proj = jnp.dot(normed_in, w_k, preferred_element_type=jnp.float32)
    value_proj = jnp.dot(normed_in, w_v, preferred_element_type=jnp.float32)
    token_pos = seq_index * tok_rows + jnp.arange(tok_rows, dtype=jnp.int32)
    doc_ends = jnp.cumsum(doc_lengths)
    doc_starts = doc_ends - doc_lengths
    doc_start = jnp.max(
        jnp.where(doc_starts[None, :] <= token_pos[:, None], doc_starts[None, :], 0), axis=1
    )
    positions = token_pos - doc_start
    rotated_q = rotate(queries.reshape(tok_rows, q_local, HEAD_DIM), positions).astype(jnp.bfloat16)
    rotated_q = rotated_q.reshape(tok_rows, kv_local, group_size, HEAD_DIM)
    rotated_k = rotate(key_proj.reshape(tok_rows, kv_local, HEAD_DIM), positions).astype(
        jnp.bfloat16
    )
    packed = jnp.concatenate(
        [rotated_k.reshape(tok_rows, key_width), value_proj.astype(jnp.bfloat16)], axis=1
    )
    earliest = doc_start[0]
    latest = token_pos[tok_rows - 1]
    initial = (
        jnp.full((kv_local, group_size, tok_rows), NEG_FILL, jnp.float32),
        jnp.zeros((kv_local, group_size, tok_rows), jnp.float32),
        jnp.zeros((kv_local, group_size, tok_rows, HEAD_DIM), jnp.float32),
    )
    shard_rows = lax.all_gather(packed, ("z", "y"), axis=0, tiled=True)
    offset = jnp.int32(0)
    row_count = shard_rows.shape[0]
    key_pos = jnp.arange(row_count, dtype=jnp.int32)

    def update(current):
        top_score, totals, context_sum = current
        key_rows = shard_rows[:, :key_width].reshape(row_count, kv_local, HEAD_DIM)
        value_rows = shard_rows[:, key_width:].reshape(row_count, kv_local, HEAD_DIM)
        scores = (
            jnp.einsum("tkgd,skd->kgts", rotated_q, key_rows, preferred_element_type=jnp.float32)
            * ATTN_SCALE
        )
        allowed = (key_pos[None, :] >= doc_start[:, None]) & (
            key_pos[None, :] <= token_pos[:, None]
        )
        scores = jnp.where(allowed, scores, NEG_FILL)
        new_top = jnp.maximum(top_score, jnp.max(scores, axis=-1))
        weights = jnp.where(allowed, jnp.exp(scores - new_top[..., None]), 0.0)
        rescale = jnp.exp(top_score - new_top)
        totals = jnp.sum(weights, axis=-1)
        context_sum = jnp.einsum(
            "kgts,skd->kgtd",
            weights.astype(jnp.bfloat16),
            value_rows,
            preferred_element_type=jnp.float32,
        )
        return (new_top, totals, context_sum)

    skip_piece = (offset + row_count <= earliest) | (offset > latest)
    top_score, totals, context_sum = lax.cond(skip_piece, lambda current: current, update, initial)
    context = (
        (context_sum / totals[..., None])
        .transpose(2, 0, 1, 3)
        .reshape(tok_rows, q_local * HEAD_DIM)
        .astype(jnp.bfloat16)
    )
    vocab_local = w_head.shape[1]
    y_count = lax.psum(1, "y")
    z_count = lax.psum(1, "z")
    z_index = lax.axis_index("z")
    y_index = lax.axis_index("y")
    kv_index = lax.axis_index("kv")
    kv_count = lax.psum(1, "kv")
    kv_bits = kv_count.bit_length() - 1
    partial = jnp.dot(context, w_o, preferred_element_type=jnp.float32)
    chunk = tok_rows // kv_count
    blocks = partial.reshape((2,) * kv_bits + (chunk, partial.shape[1]))
    for bit in range(kv_bits):
        mine_low = (kv_index >> bit) % 2 == 0
        axis = kv_bits - 1 - bit
        low = lax.index_in_dim(blocks, 0, axis, keepdims=False)
        high = lax.index_in_dim(blocks, 1, axis, keepdims=False)
        keep = jnp.where(mine_low, low, high)
        send = jnp.where(mine_low, high, low)
        got = lax.ppermute(send, "kv", [(p, p ^ (1 << bit)) for p in range(kv_count)])
        blocks = jnp.where(mine_low, keep + got, got + keep)
    attn_part = blocks
    stream_part = lax.dynamic_slice_in_dim(stream, kv_index * chunk, chunk, 0)
    final_part = rms_norm(stream_part + RESID_SCALE * attn_part, final_gain).astype(jnp.bfloat16)
    rows = final_part[None]
    for bit in reversed(range(kv_bits)):
        mine_low = (kv_index >> bit) % 2 == 0
        got = lax.ppermute(rows, "kv", [(p, p ^ (1 << bit)) for p in range(kv_count)])
        rows = jnp.where(mine_low, jnp.stack([rows, got], axis=1), jnp.stack([got, rows], axis=1))
        rows = rows.reshape((rows.shape[0] * 2,) + rows.shape[2:])
    final_in = rows.reshape(tok_rows, final_part.shape[1])
    head_rows = lax.all_gather(final_in, "y", axis=0, tiled=True)
    group_rows = head_rows.shape[0]
    head_pad = jnp.zeros((16 - 1, vocab_local), w_head.dtype)
    head_ext = jnp.concatenate([w_head, vocab_mask.astype(w_head.dtype)[None, :], head_pad], axis=0)
    head_ext = lax.all_gather(head_ext, "z", axis=1, tiled=True)
    head_cols = head_ext[: w_head.shape[0]]
    mask_cols = head_ext[w_head.shape[0]]
    live_mask = mask_cols == 1.0
    shard_ids = kv_index * (z_count * y_count) + jnp.arange(z_count, dtype=jnp.int32) * y_count + y_index
    columns = (shard_ids[:, None] * vocab_local + jnp.arange(vocab_local, dtype=jnp.int32)[None, :]).reshape(-1)
    row_ids = lax.dynamic_slice_in_dim(target_ids, z_index * group_rows, group_rows, 0)
    logits = jnp.dot(head_rows, head_cols, preferred_element_type=jnp.float32) * LOGIT_SCALE
    masked = jnp.where(live_mask[None, :], logits, NEG_FILL)
    top_row = jnp.max(masked, axis=1)
    shifted = jnp.where(live_mask[None, :], masked - top_row[:, None], 0.0)
    expw = jnp.where(live_mask[None, :], jnp.exp(shifted), 0.0)
    target = jnp.sum(jnp.where(row_ids[:, None] == columns[None, :], logits, 0.0), axis=1)
    row_stats = jnp.stack(
        [top_row, jnp.sum(expw, axis=1), jnp.sum(expw * shifted, axis=1), target]
    ).reshape(4, y_count, tok_rows)
    half = y_count // 2
    my_half = y_index // half
    keep = lax.dynamic_slice_in_dim(row_stats, my_half * half, half, 1)
    send = lax.dynamic_slice_in_dim(row_stats, (1 - my_half) * half, half, 1)
    got = lax.ppermute(send, "y", [(p, p ^ half) for p in range(y_count)])
    merged = merge_stats(keep, got, my_half == 0)
    width = half
    while width > 1:
        width //= 2
        my_part = (y_index // width) % 2
        keep = lax.dynamic_slice_in_dim(merged, my_part * width, width, 1)
        send = lax.dynamic_slice_in_dim(merged, (1 - my_part) * width, width, 1)
        got = lax.ppermute(send, "y", [(p, p ^ width) for p in range(y_count)])
        merged = merge_stats(keep, got, my_part == 0)
    merged = merged[:, 0]
    step = 1
    while step < kv_count:
        got = lax.ppermute(merged, "kv", [(p, p ^ step) for p in range(kv_count)])
        merged = merge_stats(merged, got, (kv_index // step) % 2 == 0)
        step *= 2
    top_all, total_all, spread_all, target_all = merged[0], merged[1], merged[2], merged[3]
    log_probs = target_all - top_all - jnp.log(total_all)
    entropies = jnp.log(total_all) - spread_all / total_all
    return (log_probs, entropies)


def solution(mesh):
    kv_size, seq_size = mesh.devices.shape
    z_size = mesh.shape["seq"] // 4 if mesh.shape["seq"] % 4 == 0 else mesh.shape["seq"]
    y_size = seq_size // z_size
    split_mesh = Mesh(mesh.devices.reshape(kv_size, z_size, y_size), ("kv", "z", "y"))
    seq = ("z", "y")
    in_specs = (
        P(seq, None),
        P(),
        P(None, "kv"),
        P(None, "kv"),
        P(None, "kv"),
        P("kv", None),
        P(),
        P(None, ("kv",) + seq),
        P(),
        P(),
        P(("kv",) + seq),
    )
    out_specs = (P(seq), P(seq))
    return jax.shard_map(local, mesh=split_mesh, in_specs=in_specs, out_specs=out_specs, check_vma=False)
```

```python
import math

import jax
import jax.numpy as jnp
from jax import lax
from jax.sharding import Mesh, PartitionSpec as P

HEAD_DIM = 64


ROPE_THETA = 10000000.0
NORM_EPS = 1e-05
NEG_FILL = -1e30
ATTN_SCALE = 0.015625
RESID_SCALE = 5.0
LOGIT_SCALE = 0.125


def rms_norm(values, gain_vec):
    return (
        values * lax.rsqrt(jnp.mean(values * values, axis=-1, keepdims=True) + NORM_EPS) * gain_vec
    )


def rotate(values, positions):
    half_dim = values.shape[-1] // 2
    inverse = jnp.exp(
        jnp.arange(half_dim, dtype=jnp.float32) * (-2.0 * math.log(ROPE_THETA) / values.shape[-1])
    )
    angles = positions.astype(jnp.float32)[:, None] * inverse[None, :]
    cos_val = jnp.cos(angles)[:, None, :]
    sine_val = jnp.sin(angles)[:, None, :]
    lower_half = values[..., :half_dim]
    upper_half = values[..., half_dim:]
    return jnp.concatenate(
        [
            lower_half * cos_val - upper_half * sine_val,
            upper_half * cos_val + lower_half * sine_val,
        ],
        axis=-1,
    )


def merge_stats(mine, other, mine_first):
    first = jnp.where(mine_first, mine, other)
    second = jnp.where(mine_first, other, mine)
    top = jnp.maximum(first[0], second[0])
    gap_a = first[0] - top
    gap_b = second[0] - top
    scale_a = jnp.exp(gap_a)
    scale_b = jnp.exp(gap_b)
    total = first[1] * scale_a + second[1] * scale_b
    spread = scale_a * (first[2] + gap_a * first[1]) + scale_b * (second[2] + gap_b * second[1])
    target = first[3] + second[3]
    return jnp.stack([top, total, spread, target])


def local(
    hidden_states,
    attn_gain,
    w_q,
    w_k,
    w_v,
    w_o,
    final_gain,
    w_head,
    doc_lengths,
    target_ids,
    vocab_mask,
):
    tok_rows = hidden_states.shape[0]
    seq_index = lax.axis_index(("z", "y"))
    kv_local = w_k.shape[1] // HEAD_DIM
    q_local = w_q.shape[1] // HEAD_DIM
    group_size = q_local // kv_local
    key_width = kv_local * HEAD_DIM
    stream = hidden_states.astype(jnp.float32)
    normed_in = rms_norm(stream, attn_gain).astype(jnp.bfloat16)
    queries = jnp.dot(normed_in, w_q, preferred_element_type=jnp.float32)
    key_proj = jnp.dot(normed_in, w_k, preferred_element_type=jnp.float32)
    value_proj = jnp.dot(normed_in, w_v, preferred_element_type=jnp.float32)
    token_pos = seq_index * tok_rows + jnp.arange(tok_rows, dtype=jnp.int32)
    doc_ends = jnp.cumsum(doc_lengths)
    doc_starts = doc_ends - doc_lengths
    doc_start = jnp.max(
        jnp.where(doc_starts[None, :] <= token_pos[:, None], doc_starts[None, :], 0), axis=1
    )
    positions = token_pos - doc_start
    rotated_q = rotate(queries.reshape(tok_rows, q_local, HEAD_DIM), positions).astype(jnp.bfloat16)
    rotated_q = rotated_q.reshape(tok_rows, kv_local, group_size, HEAD_DIM)
    rotated_k = rotate(key_proj.reshape(tok_rows, kv_local, HEAD_DIM), positions).astype(
        jnp.bfloat16
    )
    packed = jnp.concatenate(
        [rotated_k.reshape(tok_rows, key_width), value_proj.astype(jnp.bfloat16)], axis=1
    )
    earliest = doc_start[0]
    latest = token_pos[tok_rows - 1]
    initial = (
        jnp.full((kv_local, group_size, tok_rows), NEG_FILL, jnp.float32),
        jnp.zeros((kv_local, group_size, tok_rows), jnp.float32),
        jnp.zeros((kv_local, group_size, tok_rows, HEAD_DIM), jnp.float32),
    )
    z_count = lax.psum(1, "z")
    y_count = lax.psum(1, "y")
    z_bits = z_count.bit_length() - 1
    y_bits = y_count.bit_length() - 1
    z_pos = lax.axis_index("z")
    y_pos = lax.axis_index("y")
    gathered = packed.reshape((1,) * (z_bits + y_bits) + packed.shape)
    order = [("z", bit, z_pos, z_count, z_bits - 1 - bit) for bit in range(z_bits)]
    order += [("y", bit, y_pos, y_count, z_bits + y_bits - 1 - bit) for bit in range(y_bits)]
    for name, bit, pos, count, axis in order:
        mine_low = (pos >> bit) % 2 == 0
        got = lax.ppermute(gathered, name, [(p, p ^ (1 << bit)) for p in range(count)])
        gathered = jnp.where(
            mine_low,
            jnp.concatenate([gathered, got], axis=axis),
            jnp.concatenate([got, gathered], axis=axis),
        )
    shard_rows = gathered.reshape((-1,) + packed.shape[1:])
    offset = jnp.int32(0)
    row_count = shard_rows.shape[0]
    key_pos = jnp.arange(row_count, dtype=jnp.int32)

    def update(current):
        top_score, totals, context_sum = current
        key_rows = shard_rows[:, :key_width].reshape(row_count, kv_local, HEAD_DIM)
        value_rows = shard_rows[:, key_width:].reshape(row_count, kv_local, HEAD_DIM)
        scores = (
            jnp.einsum("tkgd,skd->kgts", rotated_q, key_rows, preferred_element_type=jnp.float32)
            * ATTN_SCALE
        )
        allowed = (key_pos[None, :] >= doc_start[:, None]) & (
            key_pos[None, :] <= token_pos[:, None]
        )
        scores = jnp.where(allowed, scores, NEG_FILL)
        new_top = jnp.maximum(top_score, jnp.max(scores, axis=-1))
        weights = jnp.where(allowed, jnp.exp(scores - new_top[..., None]), 0.0)
        rescale = jnp.exp(top_score - new_top)
        totals = jnp.sum(weights, axis=-1)
        context_sum = jnp.einsum(
            "kgts,skd->kgtd",
            weights.astype(jnp.bfloat16),
            value_rows,
            preferred_element_type=jnp.float32,
        )
        return (new_top, totals, context_sum)

    skip_piece = (offset + row_count <= earliest) | (offset > latest)
    top_score, totals, context_sum = lax.cond(skip_piece, lambda current: current, update, initial)
    context = (
        (context_sum / totals[..., None])
        .transpose(2, 0, 1, 3)
        .reshape(tok_rows, q_local * HEAD_DIM)
        .astype(jnp.bfloat16)
    )
    vocab_local = w_head.shape[1]
    z_index = lax.axis_index("z")
    y_index = lax.axis_index("y")
    kv_index = lax.axis_index("kv")
    kv_count = lax.psum(1, "kv")
    kv_bits = kv_count.bit_length() - 1
    partial = jnp.dot(context, w_o, preferred_element_type=jnp.float32)
    chunk = tok_rows // kv_count
    blocks = partial.reshape((2,) * kv_bits + (chunk, partial.shape[1]))
    for bit in range(kv_bits):
        mine_low = (kv_index >> bit) % 2 == 0
        axis = kv_bits - 1 - bit
        low = lax.index_in_dim(blocks, 0, axis, keepdims=False)
        high = lax.index_in_dim(blocks, 1, axis, keepdims=False)
        keep = jnp.where(mine_low, low, high)
        send = jnp.where(mine_low, high, low)
        got = lax.ppermute(send, "kv", [(p, p ^ (1 << bit)) for p in range(kv_count)])
        blocks = jnp.where(mine_low, keep + got, got + keep)
    attn_part = blocks
    stream_part = lax.dynamic_slice_in_dim(stream, kv_index * chunk, chunk, 0)
    final_part = rms_norm(stream_part + RESID_SCALE * attn_part, final_gain).astype(jnp.bfloat16)
    rows = final_part[None]
    for bit in reversed(range(kv_bits)):
        mine_low = (kv_index >> bit) % 2 == 0
        got = lax.ppermute(rows, "kv", [(p, p ^ (1 << bit)) for p in range(kv_count)])
        rows = jnp.where(mine_low, jnp.stack([rows, got], axis=1), jnp.stack([got, rows], axis=1))
        rows = rows.reshape((rows.shape[0] * 2,) + rows.shape[2:])
    final_in = rows.reshape(tok_rows, final_part.shape[1])
    head_rows = lax.all_gather(final_in, "y", axis=0, tiled=True)
    group_rows = head_rows.shape[0]
    padded_local = -(-vocab_local // 16) * 16
    head_pad = jnp.zeros((16 - 1, vocab_local), w_head.dtype)
    head_ext = jnp.concatenate([w_head, vocab_mask.astype(w_head.dtype)[None, :], head_pad], axis=0)
    head_ext = jnp.pad(head_ext, ((0, 0), (0, padded_local - vocab_local)))
    head_ext = lax.all_gather(head_ext, "z", axis=1, tiled=True)
    head_cols = head_ext[: w_head.shape[0]]
    mask_cols = head_ext[w_head.shape[0]]
    live_mask = mask_cols == 1.0
    shard_ids = kv_index * (z_count * y_count) + jnp.arange(z_count, dtype=jnp.int32) * y_count + y_index
    local_cols = jnp.arange(padded_local, dtype=jnp.int32)
    columns = jnp.where(
        local_cols[None, :] < vocab_local, shard_ids[:, None] * vocab_local + local_cols[None, :], -1
    ).reshape(-1)
    row_ids = lax.dynamic_slice_in_dim(target_ids, z_index * group_rows, group_rows, 0)
    logits = jnp.dot(head_rows, head_cols, preferred_element_type=jnp.float32) * LOGIT_SCALE
    masked = jnp.where(live_mask[None, :], logits, NEG_FILL)
    top_row = jnp.max(masked, axis=1)
    shifted = jnp.where(live_mask[None, :], masked - top_row[:, None], 0.0)
    expw = jnp.where(live_mask[None, :], jnp.exp(shifted), 0.0)
    target = jnp.sum(jnp.where(row_ids[:, None] == columns[None, :], logits, 0.0), axis=1)
    row_stats = jnp.stack(
        [top_row, jnp.sum(expw, axis=1), jnp.sum(expw * shifted, axis=1), target]
    ).reshape(4, y_count, tok_rows)
    half = y_count // 2
    my_half = y_index // half
    keep = lax.dynamic_slice_in_dim(row_stats, my_half * half, half, 1)
    send = lax.dynamic_slice_in_dim(row_stats, (1 - my_half) * half, half, 1)
    got = lax.ppermute(send, "y", [(p, p ^ half) for p in range(y_count)])
    merged = merge_stats(keep, got, my_half == 0)
    width = half
    while width > 1:
        width //= 2
        my_part = (y_index // width) % 2
        keep = lax.dynamic_slice_in_dim(merged, my_part * width, width, 1)
        send = lax.dynamic_slice_in_dim(merged, (1 - my_part) * width, width, 1)
        got = lax.ppermute(send, "y", [(p, p ^ width) for p in range(y_count)])
        merged = merge_stats(keep, got, my_part == 0)
    merged = merged[:, 0]
    step = 1
    while step < kv_count:
        got = lax.ppermute(merged, "kv", [(p, p ^ step) for p in range(kv_count)])
        merged = merge_stats(merged, got, (kv_index // step) % 2 == 0)
        step *= 2
    top_all, total_all, spread_all, target_all = merged[0], merged[1], merged[2], merged[3]
    log_probs = target_all - top_all - jnp.log(total_all)
    entropies = jnp.log(total_all) - spread_all / total_all
    return (log_probs, entropies)


def solution(mesh):
    kv_size, seq_size = mesh.devices.shape
    z_size = mesh.shape["seq"] // 4 if mesh.shape["seq"] % 4 == 0 else mesh.shape["seq"]
    y_size = seq_size // z_size
    split_mesh = Mesh(mesh.devices.reshape(kv_size, z_size, y_size), ("kv", "z", "y"))
    seq = ("z", "y")
    in_specs = (
        P(seq, None),
        P(),
        P(None, "kv"),
        P(None, "kv"),
        P(None, "kv"),
        P("kv", None),
        P(),
        P(None, ("kv",) + seq),
        P(),
        P(),
        P(("kv",) + seq),
    )
    out_specs = (P(seq), P(seq))
    return jax.shard_map(local, mesh=split_mesh, in_specs=in_specs, out_specs=out_specs, check_vma=False)
```

```python
import math

import jax
import jax.numpy as jnp
from jax import lax
from jax.sharding import Mesh, PartitionSpec as P

HEAD_DIM = 64


ROPE_THETA = 10000000.0
NORM_EPS = 1e-05
NEG_FILL = -1e30
ATTN_SCALE = 0.015625
RESID_SCALE = 5.0
LOGIT_SCALE = 0.125


def rms_norm(values, gain_vec):
    return (
        values * lax.rsqrt(jnp.mean(values * values, axis=-1, keepdims=True) + NORM_EPS) * gain_vec
    )


def rotate(values, positions):
    half_dim = values.shape[-1] // 2
    inverse = jnp.exp(
        jnp.arange(half_dim, dtype=jnp.float32) * (-2.0 * math.log(ROPE_THETA) / values.shape[-1])
    )
    angles = positions.astype(jnp.float32)[:, None] * inverse[None, :]
    cos_val = jnp.cos(angles)[:, None, :]
    sine_val = jnp.sin(angles)[:, None, :]
    lower_half = values[..., :half_dim]
    upper_half = values[..., half_dim:]
    return jnp.concatenate(
        [
            lower_half * cos_val - upper_half * sine_val,
            upper_half * cos_val + lower_half * sine_val,
        ],
        axis=-1,
    )


def merge_stats(mine, other, mine_first):
    first = jnp.where(mine_first, mine, other)
    second = jnp.where(mine_first, other, mine)
    top = jnp.maximum(first[0], second[0])
    gap_a = first[0] - top
    gap_b = second[0] - top
    scale_a = jnp.exp(gap_a)
    scale_b = jnp.exp(gap_b)
    total = first[1] * scale_a + second[1] * scale_b
    spread = scale_a * (first[2] + gap_a * first[1]) + scale_b * (second[2] + gap_b * second[1])
    target = first[3] + second[3]
    return jnp.stack([top, total, spread, target])


def local(
    hidden_states,
    attn_gain,
    w_q,
    w_k,
    w_v,
    w_o,
    final_gain,
    w_head,
    doc_lengths,
    target_ids,
    vocab_mask,
):
    tok_rows = hidden_states.shape[0]
    seq_index = lax.axis_index(("z", "y"))
    kv_local = w_k.shape[1] // HEAD_DIM
    q_local = w_q.shape[1] // HEAD_DIM
    group_size = q_local // kv_local
    key_width = kv_local * HEAD_DIM
    stream = hidden_states.astype(jnp.float32)
    normed_in = rms_norm(stream, attn_gain).astype(jnp.bfloat16)
    queries = jnp.dot(normed_in, w_q, preferred_element_type=jnp.float32)
    key_proj = jnp.dot(normed_in, w_k, preferred_element_type=jnp.float32)
    value_proj = jnp.dot(normed_in, w_v, preferred_element_type=jnp.float32)
    token_pos = seq_index * tok_rows + jnp.arange(tok_rows, dtype=jnp.int32)
    doc_ends = jnp.cumsum(doc_lengths)
    doc_starts = doc_ends - doc_lengths
    doc_start = jnp.max(
        jnp.where(doc_starts[None, :] <= token_pos[:, None], doc_starts[None, :], 0), axis=1
    )
    positions = token_pos - doc_start
    rotated_q = rotate(queries.reshape(tok_rows, q_local, HEAD_DIM), positions).astype(jnp.bfloat16)
    rotated_q = rotated_q.reshape(tok_rows, kv_local, group_size, HEAD_DIM)
    rotated_k = rotate(key_proj.reshape(tok_rows, kv_local, HEAD_DIM), positions).astype(
        jnp.bfloat16
    )
    packed = jnp.concatenate(
        [rotated_k.reshape(tok_rows, key_width), value_proj.astype(jnp.bfloat16)], axis=1
    )
    initial = (
        jnp.full((kv_local, group_size, tok_rows), NEG_FILL, jnp.float32),
        jnp.zeros((kv_local, group_size, tok_rows), jnp.float32),
        jnp.zeros((kv_local, group_size, tok_rows, HEAD_DIM), jnp.float32),
    )
    z_count = lax.psum(1, "z")
    y_count = lax.psum(1, "y")
    y_bits = y_count.bit_length() - 1
    z_pos = lax.axis_index("z")
    y_pos = lax.axis_index("y")
    plane = packed[None]
    for bit in range(y_bits):
        mine_low = (y_pos >> bit) % 2 == 0
        got = lax.ppermute(plane, "y", [(p, p ^ (1 << bit)) for p in range(y_count)])
        plane = jnp.where(
            mine_low, jnp.concatenate([plane, got], axis=0), jnp.concatenate([got, plane], axis=0)
        )
    plane_rows = y_count * tok_rows
    plane = plane.reshape(plane_rows, packed.shape[1])
    max_doc = (z_count * plane_rows) // 2
    back = min(-(-(max_doc - 1) // plane_rows), z_count - 1)
    held = plane[None]
    while held.shape[0] < back + 1:
        need = min(held.shape[0], back + 1 - held.shape[0])
        got = lax.ppermute(held[:need], "z", [(p, (p + need) % z_count) for p in range(z_count)])
        held = jnp.concatenate([got, held], axis=0)
    shard_rows = held.reshape(-1, packed.shape[1])
    plane_ids = (z_pos - back + jnp.arange(back + 1, dtype=jnp.int32)) % z_count
    key_pos = (plane_ids[:, None] * plane_rows + jnp.arange(plane_rows, dtype=jnp.int32)[None, :]).reshape(-1)
    row_count = shard_rows.shape[0]

    def update(current):
        top_score, totals, context_sum = current
        key_rows = shard_rows[:, :key_width].reshape(row_count, kv_local, HEAD_DIM)
        value_rows = shard_rows[:, key_width:].reshape(row_count, kv_local, HEAD_DIM)
        scores = (
            jnp.einsum("tkgd,skd->kgts", rotated_q, key_rows, preferred_element_type=jnp.float32)
            * ATTN_SCALE
        )
        allowed = (key_pos[None, :] >= doc_start[:, None]) & (
            key_pos[None, :] <= token_pos[:, None]
        )
        scores = jnp.where(allowed, scores, NEG_FILL)
        new_top = jnp.maximum(top_score, jnp.max(scores, axis=-1))
        weights = jnp.where(allowed, jnp.exp(scores - new_top[..., None]), 0.0)
        rescale = jnp.exp(top_score - new_top)
        totals = jnp.sum(weights, axis=-1)
        context_sum = jnp.einsum(
            "kgts,skd->kgtd",
            weights.astype(jnp.bfloat16),
            value_rows,
            preferred_element_type=jnp.float32,
        )
        return (new_top, totals, context_sum)

    top_score, totals, context_sum = update(initial)
    context = (
        (context_sum / totals[..., None])
        .transpose(2, 0, 1, 3)
        .reshape(tok_rows, q_local * HEAD_DIM)
        .astype(jnp.bfloat16)
    )
    vocab_local = w_head.shape[1]
    z_index = lax.axis_index("z")
    y_index = lax.axis_index("y")
    kv_index = lax.axis_index("kv")
    kv_count = lax.psum(1, "kv")
    kv_bits = kv_count.bit_length() - 1
    partial = jnp.dot(context, w_o, preferred_element_type=jnp.float32)
    chunk = tok_rows // kv_count
    blocks = partial.reshape((2,) * kv_bits + (chunk, partial.shape[1]))
    for bit in range(kv_bits):
        mine_low = (kv_index >> bit) % 2 == 0
        axis = kv_bits - 1 - bit
        low = lax.index_in_dim(blocks, 0, axis, keepdims=False)
        high = lax.index_in_dim(blocks, 1, axis, keepdims=False)
        keep = jnp.where(mine_low, low, high)
        send = jnp.where(mine_low, high, low)
        got = lax.ppermute(send, "kv", [(p, p ^ (1 << bit)) for p in range(kv_count)])
        blocks = jnp.where(mine_low, keep + got, got + keep)
    attn_part = blocks
    stream_part = lax.dynamic_slice_in_dim(stream, kv_index * chunk, chunk, 0)
    final_part = rms_norm(stream_part + RESID_SCALE * attn_part, final_gain).astype(jnp.bfloat16)
    rows = final_part[None]
    for bit in reversed(range(kv_bits)):
        mine_low = (kv_index >> bit) % 2 == 0
        got = lax.ppermute(rows, "kv", [(p, p ^ (1 << bit)) for p in range(kv_count)])
        rows = jnp.where(mine_low, jnp.stack([rows, got], axis=1), jnp.stack([got, rows], axis=1))
        rows = rows.reshape((rows.shape[0] * 2,) + rows.shape[2:])
    final_in = rows.reshape(tok_rows, final_part.shape[1])
    head_rows = lax.all_gather(final_in, "y", axis=0, tiled=True)
    group_rows = head_rows.shape[0]
    padded_local = -(-vocab_local // 16) * 16
    head_pad = jnp.zeros((16 - 1, vocab_local), w_head.dtype)
    head_ext = jnp.concatenate([w_head, vocab_mask.astype(w_head.dtype)[None, :], head_pad], axis=0)
    head_ext = jnp.pad(head_ext, ((0, 0), (0, padded_local - vocab_local)))
    head_ext, shard_rows = lax.optimization_barrier((head_ext, shard_rows))
    head_ext = lax.all_gather(head_ext, "z", axis=1, tiled=True)
    head_cols = head_ext[: w_head.shape[0]]
    mask_cols = head_ext[w_head.shape[0]]
    live_mask = mask_cols == 1.0
    shard_ids = kv_index * (z_count * y_count) + jnp.arange(z_count, dtype=jnp.int32) * y_count + y_index
    local_cols = jnp.arange(padded_local, dtype=jnp.int32)
    columns = jnp.where(
        local_cols[None, :] < vocab_local, shard_ids[:, None] * vocab_local + local_cols[None, :], -1
    ).reshape(-1)
    row_ids = lax.dynamic_slice_in_dim(target_ids, z_index * group_rows, group_rows, 0)
    logits = jnp.dot(head_rows, head_cols, preferred_element_type=jnp.float32) * LOGIT_SCALE
    masked = jnp.where(live_mask[None, :], logits, NEG_FILL)
    top_row = jnp.max(masked, axis=1)
    shifted = jnp.where(live_mask[None, :], masked - top_row[:, None], 0.0)
    expw = jnp.where(live_mask[None, :], jnp.exp(shifted), 0.0)
    target = jnp.sum(jnp.where(row_ids[:, None] == columns[None, :], logits, 0.0), axis=1)
    row_stats = jnp.stack(
        [top_row, jnp.sum(expw, axis=1), jnp.sum(expw * shifted, axis=1), target]
    ).reshape(4, y_count, tok_rows)
    half = y_count // 2
    my_half = y_index // half
    keep = lax.dynamic_slice_in_dim(row_stats, my_half * half, half, 1)
    send = lax.dynamic_slice_in_dim(row_stats, (1 - my_half) * half, half, 1)
    got = lax.ppermute(send, "y", [(p, p ^ half) for p in range(y_count)])
    merged = merge_stats(keep, got, my_half == 0)
    width = half
    while width > 1:
        width //= 2
        my_part = (y_index // width) % 2
        keep = lax.dynamic_slice_in_dim(merged, my_part * width, width, 1)
        send = lax.dynamic_slice_in_dim(merged, (1 - my_part) * width, width, 1)
        got = lax.ppermute(send, "y", [(p, p ^ width) for p in range(y_count)])
        merged = merge_stats(keep, got, my_part == 0)
    merged = merged[:, 0]
    step = 1
    while step < kv_count:
        got = lax.ppermute(merged, "kv", [(p, p ^ step) for p in range(kv_count)])
        merged = merge_stats(merged, got, (kv_index // step) % 2 == 0)
        step *= 2
    top_all, total_all, spread_all, target_all = merged[0], merged[1], merged[2], merged[3]
    log_probs = target_all - top_all - jnp.log(total_all)
    entropies = jnp.log(total_all) - spread_all / total_all
    return (log_probs, entropies)


def solution(mesh):
    kv_size, seq_size = mesh.devices.shape
    z_size = mesh.shape["seq"] // 4 if mesh.shape["seq"] % 4 == 0 else mesh.shape["seq"]
    y_size = seq_size // z_size
    split_mesh = Mesh(mesh.devices.reshape(kv_size, z_size, y_size), ("kv", "z", "y"))
    seq = ("z", "y")
    in_specs = (
        P(seq, None),
        P(),
        P(None, "kv"),
        P(None, "kv"),
        P(None, "kv"),
        P("kv", None),
        P(),
        P(None, ("kv",) + seq),
        P(),
        P(),
        P(("kv",) + seq),
    )
    out_specs = (P(seq), P(seq))
    return jax.shard_map(local, mesh=split_mesh, in_specs=in_specs, out_specs=out_specs, check_vma=False)
```

```python
import math

import jax
import jax.numpy as jnp
from jax import lax
from jax.sharding import Mesh, PartitionSpec as P

HEAD_DIM = 64


ROPE_THETA = 10000000.0
NORM_EPS = 1e-05
NEG_FILL = -1e30
ATTN_SCALE = 0.015625
RESID_SCALE = 5.0
LOGIT_SCALE = 0.125


def rms_norm(values, gain_vec):
    return (
        values * lax.rsqrt(jnp.mean(values * values, axis=-1, keepdims=True) + NORM_EPS) * gain_vec
    )


def rotate(values, positions):
    half_dim = values.shape[-1] // 2
    inverse = jnp.exp(
        jnp.arange(half_dim, dtype=jnp.float32) * (-2.0 * math.log(ROPE_THETA) / values.shape[-1])
    )
    angles = positions.astype(jnp.float32)[:, None] * inverse[None, :]
    cos_val = jnp.cos(angles)[:, None, :]
    sine_val = jnp.sin(angles)[:, None, :]
    lower_half = values[..., :half_dim]
    upper_half = values[..., half_dim:]
    return jnp.concatenate(
        [
            lower_half * cos_val - upper_half * sine_val,
            upper_half * cos_val + lower_half * sine_val,
        ],
        axis=-1,
    )


def merge_stats(mine, other, mine_first):
    first = jnp.where(mine_first, mine, other)
    second = jnp.where(mine_first, other, mine)
    top = jnp.maximum(first[0], second[0])
    gap_a = first[0] - top
    gap_b = second[0] - top
    scale_a = jnp.exp(gap_a)
    scale_b = jnp.exp(gap_b)
    total = first[1] * scale_a + second[1] * scale_b
    spread = scale_a * (first[2] + gap_a * first[1]) + scale_b * (second[2] + gap_b * second[1])
    target = first[3] + second[3]
    return jnp.stack([top, total, spread, target])


def local(
    hidden_states,
    attn_gain,
    w_q,
    w_k,
    w_v,
    w_o,
    final_gain,
    w_head,
    doc_lengths,
    target_ids,
    vocab_mask,
):
    tok_rows = hidden_states.shape[0]
    seq_index = lax.axis_index(("z", "y"))
    kv_local = w_k.shape[1] // HEAD_DIM
    q_local = w_q.shape[1] // HEAD_DIM
    group_size = q_local // kv_local
    key_width = kv_local * HEAD_DIM
    stream = hidden_states.astype(jnp.float32)
    normed_in = rms_norm(stream, attn_gain).astype(jnp.bfloat16)
    queries = jnp.dot(normed_in, w_q, preferred_element_type=jnp.float32)
    key_proj = jnp.dot(normed_in, w_k, preferred_element_type=jnp.float32)
    value_proj = jnp.dot(normed_in, w_v, preferred_element_type=jnp.float32)
    token_pos = seq_index * tok_rows + jnp.arange(tok_rows, dtype=jnp.int32)
    doc_ends = jnp.cumsum(doc_lengths)
    doc_starts = doc_ends - doc_lengths
    doc_start = jnp.max(
        jnp.where(doc_starts[None, :] <= token_pos[:, None], doc_starts[None, :], 0), axis=1
    )
    positions = token_pos - doc_start
    rotated_q = rotate(queries.reshape(tok_rows, q_local, HEAD_DIM), positions).astype(jnp.bfloat16)
    rotated_q = rotated_q.reshape(tok_rows, kv_local, group_size, HEAD_DIM)
    rotated_k = rotate(key_proj.reshape(tok_rows, kv_local, HEAD_DIM), positions).astype(
        jnp.bfloat16
    )
    packed = jnp.concatenate(
        [rotated_k.reshape(tok_rows, key_width), value_proj.astype(jnp.bfloat16)], axis=1
    )
    initial = (
        jnp.full((kv_local, group_size, tok_rows), NEG_FILL, jnp.float32),
        jnp.zeros((kv_local, group_size, tok_rows), jnp.float32),
        jnp.zeros((kv_local, group_size, tok_rows, HEAD_DIM), jnp.float32),
    )
    z_count = lax.psum(1, "z")
    y_count = lax.psum(1, "y")
    y_bits = y_count.bit_length() - 1
    z_pos = lax.axis_index("z")
    y_pos = lax.axis_index("y")
    plane = packed[None]
    for bit in range(y_bits):
        mine_low = (y_pos >> bit) % 2 == 0
        got = lax.ppermute(plane, "y", [(p, p ^ (1 << bit)) for p in range(y_count)])
        plane = jnp.where(
            mine_low, jnp.concatenate([plane, got], axis=0), jnp.concatenate([got, plane], axis=0)
        )
    plane_rows = y_count * tok_rows
    plane = plane.reshape(plane_rows, packed.shape[1])
    max_doc = (z_count * plane_rows) // 2
    back = min(-(-(max_doc - 1) // plane_rows), z_count - 1)
    held = plane[None]
    while held.shape[0] < back + 1:
        need = min(held.shape[0], back + 1 - held.shape[0])
        got = lax.ppermute(held[:need], "z", [(p, (p + need) % z_count) for p in range(z_count)])
        held = jnp.concatenate([got, held], axis=0)
    shard_rows = held.reshape(-1, packed.shape[1])
    plane_ids = (z_pos - back + jnp.arange(back + 1, dtype=jnp.int32)) % z_count
    key_pos = (plane_ids[:, None] * plane_rows + jnp.arange(plane_rows, dtype=jnp.int32)[None, :]).reshape(-1)
    row_count = shard_rows.shape[0]

    def update(current):
        top_score, totals, context_sum = current
        key_rows = shard_rows[:, :key_width].reshape(row_count, kv_local, HEAD_DIM)
        value_rows = shard_rows[:, key_width:].reshape(row_count, kv_local, HEAD_DIM)
        scores = (
            jnp.einsum("tkgd,skd->kgts", rotated_q, key_rows, preferred_element_type=jnp.float32)
            * ATTN_SCALE
        )
        allowed = (key_pos[None, :] >= doc_start[:, None]) & (
            key_pos[None, :] <= token_pos[:, None]
        )
        scores = jnp.where(allowed, scores, NEG_FILL)
        new_top = jnp.maximum(top_score, jnp.max(scores, axis=-1))
        weights = jnp.where(allowed, jnp.exp(scores - new_top[..., None]), 0.0)
        rescale = jnp.exp(top_score - new_top)
        totals = jnp.sum(weights, axis=-1)
        context_sum = jnp.einsum(
            "kgts,skd->kgtd",
            weights.astype(jnp.bfloat16),
            value_rows,
            preferred_element_type=jnp.float32,
        )
        return (new_top, totals, context_sum)

    top_score, totals, context_sum = update(initial)
    context = (
        (context_sum / totals[..., None])
        .transpose(2, 0, 1, 3)
        .reshape(tok_rows, q_local * HEAD_DIM)
        .astype(jnp.bfloat16)
    )
    vocab_local = w_head.shape[1]
    z_index = lax.axis_index("z")
    y_index = lax.axis_index("y")
    kv_index = lax.axis_index("kv")
    kv_count = lax.psum(1, "kv")
    kv_bits = kv_count.bit_length() - 1
    partial = jnp.dot(context, w_o, preferred_element_type=jnp.float32)
    chunk = tok_rows // kv_count
    blocks = partial.reshape((2,) * kv_bits + (chunk, partial.shape[1]))
    for bit in range(kv_bits):
        mine_low = (kv_index >> bit) % 2 == 0
        axis = kv_bits - 1 - bit
        low = lax.index_in_dim(blocks, 0, axis, keepdims=False)
        high = lax.index_in_dim(blocks, 1, axis, keepdims=False)
        keep = jnp.where(mine_low, low, high)
        send = jnp.where(mine_low, high, low)
        got = lax.ppermute(send, "kv", [(p, p ^ (1 << bit)) for p in range(kv_count)])
        blocks = jnp.where(mine_low, keep + got, got + keep)
    attn_part = blocks
    stream_part = lax.dynamic_slice_in_dim(stream, kv_index * chunk, chunk, 0)
    final_part = rms_norm(stream_part + RESID_SCALE * attn_part, final_gain).astype(jnp.bfloat16)
    rows = final_part[None]
    for bit in reversed(range(kv_bits)):
        mine_low = (kv_index >> bit) % 2 == 0
        got = lax.ppermute(rows, "kv", [(p, p ^ (1 << bit)) for p in range(kv_count)])
        rows = jnp.where(mine_low, jnp.stack([rows, got], axis=1), jnp.stack([got, rows], axis=1))
        rows = rows.reshape((rows.shape[0] * 2,) + rows.shape[2:])
    final_in = rows.reshape(tok_rows, final_part.shape[1])
    head_rows = lax.all_gather(final_in, "y", axis=0, tiled=True)
    group_rows = head_rows.shape[0]
    padded_local = -(-vocab_local // 16) * 16
    head_pad = jnp.zeros((16 - 1, vocab_local), w_head.dtype)
    head_ext = jnp.concatenate([w_head, vocab_mask.astype(w_head.dtype)[None, :], head_pad], axis=0)
    head_ext = jnp.pad(head_ext, ((0, 0), (0, padded_local - vocab_local)))
    head_ext = lax.all_gather(head_ext, "z", axis=1, tiled=True)
    head_cols = head_ext[: w_head.shape[0]]
    mask_cols = head_ext[w_head.shape[0]]
    live_mask = mask_cols == 1.0
    shard_ids = kv_index * (z_count * y_count) + jnp.arange(z_count, dtype=jnp.int32) * y_count + y_index
    local_cols = jnp.arange(padded_local, dtype=jnp.int32)
    columns = jnp.where(
        local_cols[None, :] < vocab_local, shard_ids[:, None] * vocab_local + local_cols[None, :], -1
    ).reshape(-1)
    row_ids = lax.dynamic_slice_in_dim(target_ids, z_index * group_rows, group_rows, 0)
    logits = jnp.dot(head_rows, head_cols, preferred_element_type=jnp.float32) * LOGIT_SCALE
    masked = jnp.where(live_mask[None, :], logits, NEG_FILL)
    top_row = jnp.max(masked, axis=1)
    shifted = jnp.where(live_mask[None, :], masked - top_row[:, None], 0.0)
    expw = jnp.where(live_mask[None, :], jnp.exp(shifted), 0.0)
    target = jnp.sum(jnp.where(row_ids[:, None] == columns[None, :], logits, 0.0), axis=1)
    row_stats = jnp.stack(
        [top_row, jnp.sum(expw, axis=1), jnp.sum(expw * shifted, axis=1), target]
    ).reshape(4, y_count, tok_rows)
    half = y_count // 2
    my_half = y_index // half
    keep = lax.dynamic_slice_in_dim(row_stats, my_half * half, half, 1)
    send = lax.dynamic_slice_in_dim(row_stats, (1 - my_half) * half, half, 1)
    got = lax.ppermute(send, "y", [(p, p ^ half) for p in range(y_count)])
    merged = merge_stats(keep, got, my_half == 0)
    width = half
    while width > 1:
        width //= 2
        my_part = (y_index // width) % 2
        keep = lax.dynamic_slice_in_dim(merged, my_part * width, width, 1)
        send = lax.dynamic_slice_in_dim(merged, (1 - my_part) * width, width, 1)
        got = lax.ppermute(send, "y", [(p, p ^ width) for p in range(y_count)])
        merged = merge_stats(keep, got, my_part == 0)
    merged = merged[:, 0]
    step = 1
    while step < kv_count:
        got = lax.ppermute(merged, "kv", [(p, p ^ step) for p in range(kv_count)])
        merged = merge_stats(merged, got, (kv_index // step) % 2 == 0)
        step *= 2
    top_all, total_all, spread_all, target_all = merged[0], merged[1], merged[2], merged[3]
    log_probs = target_all - top_all - jnp.log(total_all)
    entropies = jnp.log(total_all) - spread_all / total_all
    return (log_probs, entropies)


def solution(mesh):
    kv_size, seq_size = mesh.devices.shape
    z_size = mesh.shape["seq"] // 4 if mesh.shape["seq"] % 4 == 0 else mesh.shape["seq"]
    y_size = seq_size // z_size
    split_mesh = Mesh(mesh.devices.reshape(kv_size, z_size, y_size), ("kv", "z", "y"))
    seq = ("z", "y")
    in_specs = (
        P(seq, None),
        P(),
        P(None, "kv"),
        P(None, "kv"),
        P(None, "kv"),
        P("kv", None),
        P(),
        P(None, ("kv",) + seq),
        P(),
        P(),
        P(("kv",) + seq),
    )
    out_specs = (P(seq), P(seq))
    return jax.shard_map(local, mesh=split_mesh, in_specs=in_specs, out_specs=out_specs, check_vma=False)
```

```python
import math

import jax
import jax.numpy as jnp
from jax import lax
from jax.sharding import Mesh, PartitionSpec as P

HEAD_DIM = 64


ROPE_THETA = 10000000.0
NORM_EPS = 1e-05
NEG_FILL = -1e30
ATTN_SCALE = 0.015625
RESID_SCALE = 5.0
LOGIT_SCALE = 0.125


def rms_norm(values, gain_vec):
    return (
        values * lax.rsqrt(jnp.mean(values * values, axis=-1, keepdims=True) + NORM_EPS) * gain_vec
    )


def rotate(values, positions):
    half_dim = values.shape[-1] // 2
    inverse = jnp.exp(
        jnp.arange(half_dim, dtype=jnp.float32) * (-2.0 * math.log(ROPE_THETA) / values.shape[-1])
    )
    angles = positions.astype(jnp.float32)[:, None] * inverse[None, :]
    cos_val = jnp.cos(angles)[:, None, :]
    sine_val = jnp.sin(angles)[:, None, :]
    lower_half = values[..., :half_dim]
    upper_half = values[..., half_dim:]
    return jnp.concatenate(
        [
            lower_half * cos_val - upper_half * sine_val,
            upper_half * cos_val + lower_half * sine_val,
        ],
        axis=-1,
    )


def merge_stats(mine, other, mine_first):
    first = jnp.where(mine_first, mine, other)
    second = jnp.where(mine_first, other, mine)
    top = jnp.maximum(first[0], second[0])
    gap_a = first[0] - top
    gap_b = second[0] - top
    scale_a = jnp.exp(gap_a)
    scale_b = jnp.exp(gap_b)
    total = first[1] * scale_a + second[1] * scale_b
    spread = scale_a * (first[2] + gap_a * first[1]) + scale_b * (second[2] + gap_b * second[1])
    target = first[3] + second[3]
    return jnp.stack([top, total, spread, target])


def merge_many(parts):
    top = jnp.max(parts[:, 0], axis=0)
    gap = parts[:, 0] - top[None]
    scale = jnp.exp(gap)
    total = jnp.sum(parts[:, 1] * scale, axis=0)
    spread = jnp.sum(scale * (parts[:, 2] + gap * parts[:, 1]), axis=0)
    target = jnp.sum(parts[:, 3], axis=0)
    return jnp.stack([top, total, spread, target])


def local(
    hidden_states,
    attn_gain,
    w_q,
    w_k,
    w_v,
    w_o,
    final_gain,
    w_head,
    doc_lengths,
    target_ids,
    vocab_mask,
):
    tok_rows = hidden_states.shape[0]
    seq_index = lax.axis_index(("z", "y"))
    kv_local = w_k.shape[1] // HEAD_DIM
    q_local = w_q.shape[1] // HEAD_DIM
    group_size = q_local // kv_local
    key_width = kv_local * HEAD_DIM
    stream = hidden_states.astype(jnp.float32)
    normed_in = rms_norm(stream, attn_gain).astype(jnp.bfloat16)
    queries = jnp.dot(normed_in, w_q, preferred_element_type=jnp.float32)
    key_proj = jnp.dot(normed_in, w_k, preferred_element_type=jnp.float32)
    value_proj = jnp.dot(normed_in, w_v, preferred_element_type=jnp.float32)
    token_pos = seq_index * tok_rows + jnp.arange(tok_rows, dtype=jnp.int32)
    doc_ends = jnp.cumsum(doc_lengths)
    doc_starts = doc_ends - doc_lengths
    doc_start = jnp.max(
        jnp.where(doc_starts[None, :] <= token_pos[:, None], doc_starts[None, :], 0), axis=1
    )
    positions = token_pos - doc_start
    rotated_q = rotate(queries.reshape(tok_rows, q_local, HEAD_DIM), positions).astype(jnp.bfloat16)
    rotated_q = rotated_q.reshape(tok_rows, kv_local, group_size, HEAD_DIM)
    rotated_k = rotate(key_proj.reshape(tok_rows, kv_local, HEAD_DIM), positions).astype(
        jnp.bfloat16
    )
    packed = jnp.concatenate(
        [rotated_k.reshape(tok_rows, key_width), value_proj.astype(jnp.bfloat16)], axis=1
    )
    initial = (
        jnp.full((kv_local, group_size, tok_rows), NEG_FILL, jnp.float32),
        jnp.zeros((kv_local, group_size, tok_rows), jnp.float32),
        jnp.zeros((kv_local, group_size, tok_rows, HEAD_DIM), jnp.float32),
    )
    z_count = lax.psum(1, "z")
    y_count = lax.psum(1, "y")
    y_bits = y_count.bit_length() - 1
    z_pos = lax.axis_index("z")
    y_pos = lax.axis_index("y")
    plane = packed[None]
    for bit in range(y_bits):
        mine_low = (y_pos >> bit) % 2 == 0
        got = lax.ppermute(plane, "y", [(p, p ^ (1 << bit)) for p in range(y_count)])
        plane = jnp.where(
            mine_low, jnp.concatenate([plane, got], axis=0), jnp.concatenate([got, plane], axis=0)
        )
    plane_rows = y_count * tok_rows
    plane = plane.reshape(plane_rows, packed.shape[1])
    max_doc = (z_count * plane_rows) // 2
    back = min(-(-(max_doc - 1) // plane_rows), z_count - 1)
    held = plane[None]
    while held.shape[0] < back + 1:
        need = min(held.shape[0], back + 1 - held.shape[0])
        got = lax.ppermute(held[:need], "z", [(p, (p + need) % z_count) for p in range(z_count)])
        held = jnp.concatenate([got, held], axis=0)
    shard_rows = held.reshape(-1, packed.shape[1])
    plane_ids = (z_pos - back + jnp.arange(back + 1, dtype=jnp.int32)) % z_count
    key_pos = (plane_ids[:, None] * plane_rows + jnp.arange(plane_rows, dtype=jnp.int32)[None, :]).reshape(-1)
    row_count = shard_rows.shape[0]

    def update(current):
        top_score, totals, context_sum = current
        key_rows = shard_rows[:, :key_width].reshape(row_count, kv_local, HEAD_DIM)
        value_rows = shard_rows[:, key_width:].reshape(row_count, kv_local, HEAD_DIM)
        scores = (
            jnp.einsum("tkgd,skd->kgts", rotated_q, key_rows, preferred_element_type=jnp.float32)
            * ATTN_SCALE
        )
        allowed = (key_pos[None, :] >= doc_start[:, None]) & (
            key_pos[None, :] <= token_pos[:, None]
        )
        scores = jnp.where(allowed, scores, NEG_FILL)
        new_top = jnp.maximum(top_score, jnp.max(scores, axis=-1))
        weights = jnp.where(allowed, jnp.exp(scores - new_top[..., None]), 0.0)
        rescale = jnp.exp(top_score - new_top)
        totals = jnp.sum(weights, axis=-1)
        context_sum = jnp.einsum(
            "kgts,skd->kgtd",
            weights.astype(jnp.bfloat16),
            value_rows,
            preferred_element_type=jnp.float32,
        )
        return (new_top, totals, context_sum)

    top_score, totals, context_sum = update(initial)
    context = (
        (context_sum / totals[..., None])
        .transpose(2, 0, 1, 3)
        .reshape(tok_rows, q_local * HEAD_DIM)
        .astype(jnp.bfloat16)
    )
    vocab_local = w_head.shape[1]
    z_index = lax.axis_index("z")
    y_index = lax.axis_index("y")
    kv_index = lax.axis_index("kv")
    kv_count = lax.psum(1, "kv")
    kv_bits = kv_count.bit_length() - 1
    partial = jnp.dot(context, w_o, preferred_element_type=jnp.float32)
    chunk = tok_rows // kv_count
    pieces = lax.all_to_all(
        partial.reshape(kv_count, chunk, partial.shape[1]), "kv", 0, 0, tiled=False
    )
    attn_part = jnp.sum(pieces, axis=0)
    stream_part = lax.dynamic_slice_in_dim(stream, kv_index * chunk, chunk, 0)
    final_part = rms_norm(stream_part + RESID_SCALE * attn_part, final_gain).astype(jnp.bfloat16)
    rows = lax.all_to_all(
        jnp.broadcast_to(final_part[None], (kv_count,) + final_part.shape), "kv", 0, 0, tiled=False
    )
    final_in = rows.reshape(tok_rows, final_part.shape[1])
    head_rows = lax.all_gather(final_in, "y", axis=0, tiled=True)
    group_rows = head_rows.shape[0]
    padded_local = -(-vocab_local // 16) * 16
    head_pad = jnp.zeros((16 - 1, vocab_local), w_head.dtype)
    head_ext = jnp.concatenate([w_head, vocab_mask.astype(w_head.dtype)[None, :], head_pad], axis=0)
    head_ext = jnp.pad(head_ext, ((0, 0), (0, padded_local - vocab_local)))
    head_ext = lax.all_gather(head_ext, "z", axis=1, tiled=True)
    head_cols = head_ext[: w_head.shape[0]]
    mask_cols = head_ext[w_head.shape[0]]
    live_mask = mask_cols == 1.0
    shard_ids = kv_index * (z_count * y_count) + jnp.arange(z_count, dtype=jnp.int32) * y_count + y_index
    local_cols = jnp.arange(padded_local, dtype=jnp.int32)
    columns = jnp.where(
        local_cols[None, :] < vocab_local, shard_ids[:, None] * vocab_local + local_cols[None, :], -1
    ).reshape(-1)
    row_ids = lax.dynamic_slice_in_dim(target_ids, z_index * group_rows, group_rows, 0)
    logits = jnp.dot(head_rows, head_cols, preferred_element_type=jnp.float32) * LOGIT_SCALE
    masked = jnp.where(live_mask[None, :], logits, NEG_FILL)
    top_row = jnp.max(masked, axis=1)
    shifted = jnp.where(live_mask[None, :], masked - top_row[:, None], 0.0)
    expw = jnp.where(live_mask[None, :], jnp.exp(shifted), 0.0)
    target = jnp.sum(jnp.where(row_ids[:, None] == columns[None, :], logits, 0.0), axis=1)
    row_stats = jnp.stack(
        [top_row, jnp.sum(expw, axis=1), jnp.sum(expw * shifted, axis=1), target]
    ).reshape(4, y_count, tok_rows)
    from_y = lax.all_to_all(row_stats.transpose(1, 0, 2), "y", 0, 0, tiled=False)
    merged = merge_many(from_y)
    from_kv = lax.all_to_all(
        jnp.broadcast_to(merged[None], (kv_count,) + merged.shape), "kv", 0, 0, tiled=False
    )
    merged = merge_many(from_kv)
    top_all, total_all, spread_all, target_all = merged[0], merged[1], merged[2], merged[3]
    log_probs = target_all - top_all - jnp.log(total_all)
    entropies = jnp.log(total_all) - spread_all / total_all
    return (log_probs, entropies)


def solution(mesh):
    kv_size, seq_size = mesh.devices.shape
    z_size = mesh.shape["seq"] // 4 if mesh.shape["seq"] % 4 == 0 else mesh.shape["seq"]
    y_size = seq_size // z_size
    split_mesh = Mesh(mesh.devices.reshape(kv_size, z_size, y_size), ("kv", "z", "y"))
    seq = ("z", "y")
    in_specs = (
        P(seq, None),
        P(),
        P(None, "kv"),
        P(None, "kv"),
        P(None, "kv"),
        P("kv", None),
        P(),
        P(None, ("kv",) + seq),
        P(),
        P(),
        P(("kv",) + seq),
    )
    out_specs = (P(seq), P(seq))
    return jax.shard_map(local, mesh=split_mesh, in_specs=in_specs, out_specs=out_specs, check_vma=False)
```

```python
import math

import jax
import jax.numpy as jnp
from jax import lax
from jax.sharding import Mesh, PartitionSpec as P

HEAD_DIM = 64


ROPE_THETA = 10000000.0
NORM_EPS = 1e-05
NEG_FILL = -1e30
ATTN_SCALE = 0.015625
RESID_SCALE = 5.0
LOGIT_SCALE = 0.125


def rms_norm(values, gain_vec):
    return (
        values * lax.rsqrt(jnp.mean(values * values, axis=-1, keepdims=True) + NORM_EPS) * gain_vec
    )


def rotate(values, positions):
    half_dim = values.shape[-1] // 2
    inverse = jnp.exp(
        jnp.arange(half_dim, dtype=jnp.float32) * (-2.0 * math.log(ROPE_THETA) / values.shape[-1])
    )
    angles = positions.astype(jnp.float32)[:, None] * inverse[None, :]
    cos_val = jnp.cos(angles)[:, None, :]
    sine_val = jnp.sin(angles)[:, None, :]
    lower_half = values[..., :half_dim]
    upper_half = values[..., half_dim:]
    return jnp.concatenate(
        [
            lower_half * cos_val - upper_half * sine_val,
            upper_half * cos_val + lower_half * sine_val,
        ],
        axis=-1,
    )


def merge_stats(mine, other, mine_first):
    first = jnp.where(mine_first, mine, other)
    second = jnp.where(mine_first, other, mine)
    top = jnp.maximum(first[0], second[0])
    gap_a = first[0] - top
    gap_b = second[0] - top
    scale_a = jnp.exp(gap_a)
    scale_b = jnp.exp(gap_b)
    total = first[1] * scale_a + second[1] * scale_b
    spread = scale_a * (first[2] + gap_a * first[1]) + scale_b * (second[2] + gap_b * second[1])
    target = first[3] + second[3]
    return jnp.stack([top, total, spread, target])


def local(
    hidden_states,
    attn_gain,
    w_q,
    w_k,
    w_v,
    w_o,
    final_gain,
    w_head,
    doc_lengths,
    target_ids,
    vocab_mask,
):
    tok_rows = hidden_states.shape[0]
    seq_index = lax.axis_index(("z", "y"))
    kv_local = w_k.shape[1] // HEAD_DIM
    q_local = w_q.shape[1] // HEAD_DIM
    group_size = q_local // kv_local
    key_width = kv_local * HEAD_DIM
    stream = hidden_states.astype(jnp.float32)
    normed_in = rms_norm(stream, attn_gain).astype(jnp.bfloat16)
    queries = jnp.dot(normed_in, w_q, preferred_element_type=jnp.float32)
    key_proj = jnp.dot(normed_in, w_k, preferred_element_type=jnp.float32)
    value_proj = jnp.dot(normed_in, w_v, preferred_element_type=jnp.float32)
    token_pos = seq_index * tok_rows + jnp.arange(tok_rows, dtype=jnp.int32)
    doc_ends = jnp.cumsum(doc_lengths)
    doc_starts = doc_ends - doc_lengths
    doc_start = jnp.max(
        jnp.where(doc_starts[None, :] <= token_pos[:, None], doc_starts[None, :], 0), axis=1
    )
    positions = token_pos - doc_start
    rotated_q = rotate(queries.reshape(tok_rows, q_local, HEAD_DIM), positions).astype(jnp.bfloat16)
    rotated_q = rotated_q.reshape(tok_rows, kv_local, group_size, HEAD_DIM)
    rotated_k = rotate(key_proj.reshape(tok_rows, kv_local, HEAD_DIM), positions).astype(
        jnp.bfloat16
    )
    packed = jnp.concatenate(
        [rotated_k.reshape(tok_rows, key_width), value_proj.astype(jnp.bfloat16)], axis=1
    )
    initial = (
        jnp.full((kv_local, group_size, tok_rows), NEG_FILL, jnp.float32),
        jnp.zeros((kv_local, group_size, tok_rows), jnp.float32),
        jnp.zeros((kv_local, group_size, tok_rows, HEAD_DIM), jnp.float32),
    )
    z_count = lax.psum(1, "z")
    y_count = lax.psum(1, "y")
    y_bits = y_count.bit_length() - 1
    z_pos = lax.axis_index("z")
    y_pos = lax.axis_index("y")
    plane_rows = y_count * tok_rows
    max_doc = (z_count * plane_rows) // 2
    back = min(-(-(max_doc - 1) // plane_rows), z_count - 1)
    held = packed[None]
    while held.shape[0] < back + 1:
        need = min(held.shape[0], back + 1 - held.shape[0])
        got = lax.ppermute(held[:need], "z", [(p, (p + need) % z_count) for p in range(z_count)])
        held = jnp.concatenate([got, held], axis=0)
    held = held[:, None]
    for bit in range(y_bits):
        mine_low = (y_pos >> bit) % 2 == 0
        got = lax.ppermute(held, "y", [(p, p ^ (1 << bit)) for p in range(y_count)])
        held = jnp.where(
            mine_low, jnp.concatenate([held, got], axis=1), jnp.concatenate([got, held], axis=1)
        )
    shard_rows = held.reshape(-1, packed.shape[1])
    plane_ids = (z_pos - back + jnp.arange(back + 1, dtype=jnp.int32)) % z_count
    key_pos = (plane_ids[:, None] * plane_rows + jnp.arange(plane_rows, dtype=jnp.int32)[None, :]).reshape(-1)
    row_count = shard_rows.shape[0]

    def update(current):
        top_score, totals, context_sum = current
        key_rows = shard_rows[:, :key_width].reshape(row_count, kv_local, HEAD_DIM)
        value_rows = shard_rows[:, key_width:].reshape(row_count, kv_local, HEAD_DIM)
        scores = (
            jnp.einsum("tkgd,skd->kgts", rotated_q, key_rows, preferred_element_type=jnp.float32)
            * ATTN_SCALE
        )
        allowed = (key_pos[None, :] >= doc_start[:, None]) & (
            key_pos[None, :] <= token_pos[:, None]
        )
        scores = jnp.where(allowed, scores, NEG_FILL)
        new_top = jnp.maximum(top_score, jnp.max(scores, axis=-1))
        weights = jnp.where(allowed, jnp.exp(scores - new_top[..., None]), 0.0)
        rescale = jnp.exp(top_score - new_top)
        totals = jnp.sum(weights, axis=-1)
        context_sum = jnp.einsum(
            "kgts,skd->kgtd",
            weights.astype(jnp.bfloat16),
            value_rows,
            preferred_element_type=jnp.float32,
        )
        return (new_top, totals, context_sum)

    top_score, totals, context_sum = update(initial)
    context = (
        (context_sum / totals[..., None])
        .transpose(2, 0, 1, 3)
        .reshape(tok_rows, q_local * HEAD_DIM)
        .astype(jnp.bfloat16)
    )
    vocab_local = w_head.shape[1]
    z_index = lax.axis_index("z")
    y_index = lax.axis_index("y")
    kv_index = lax.axis_index("kv")
    kv_count = lax.psum(1, "kv")
    kv_bits = kv_count.bit_length() - 1
    partial = jnp.dot(context, w_o, preferred_element_type=jnp.float32)
    chunk = tok_rows // kv_count
    blocks = partial.reshape((2,) * kv_bits + (chunk, partial.shape[1]))
    for bit in range(kv_bits):
        mine_low = (kv_index >> bit) % 2 == 0
        axis = kv_bits - 1 - bit
        low = lax.index_in_dim(blocks, 0, axis, keepdims=False)
        high = lax.index_in_dim(blocks, 1, axis, keepdims=False)
        keep = jnp.where(mine_low, low, high)
        send = jnp.where(mine_low, high, low)
        got = lax.ppermute(send, "kv", [(p, p ^ (1 << bit)) for p in range(kv_count)])
        blocks = jnp.where(mine_low, keep + got, got + keep)
    attn_part = blocks
    stream_part = lax.dynamic_slice_in_dim(stream, kv_index * chunk, chunk, 0)
    final_part = rms_norm(stream_part + RESID_SCALE * attn_part, final_gain).astype(jnp.bfloat16)
    rows = final_part[None]
    for bit in reversed(range(kv_bits)):
        mine_low = (kv_index >> bit) % 2 == 0
        got = lax.ppermute(rows, "kv", [(p, p ^ (1 << bit)) for p in range(kv_count)])
        rows = jnp.where(mine_low, jnp.stack([rows, got], axis=1), jnp.stack([got, rows], axis=1))
        rows = rows.reshape((rows.shape[0] * 2,) + rows.shape[2:])
    final_in = rows.reshape(tok_rows, final_part.shape[1])
    head_rows = lax.all_gather(final_in, "y", axis=0, tiled=True)
    group_rows = head_rows.shape[0]
    padded_local = -(-vocab_local // 16) * 16
    head_pad = jnp.zeros((16 - 1, vocab_local), w_head.dtype)
    head_ext = jnp.concatenate([w_head, vocab_mask.astype(w_head.dtype)[None, :], head_pad], axis=0)
    head_ext = jnp.pad(head_ext, ((0, 0), (0, padded_local - vocab_local)))
    head_ext = lax.all_gather(head_ext, "z", axis=1, tiled=True)
    head_cols = head_ext[: w_head.shape[0]]
    mask_cols = head_ext[w_head.shape[0]]
    live_mask = mask_cols == 1.0
    shard_ids = kv_index * (z_count * y_count) + jnp.arange(z_count, dtype=jnp.int32) * y_count + y_index
    local_cols = jnp.arange(padded_local, dtype=jnp.int32)
    columns = jnp.where(
        local_cols[None, :] < vocab_local, shard_ids[:, None] * vocab_local + local_cols[None, :], -1
    ).reshape(-1)
    row_ids = lax.dynamic_slice_in_dim(target_ids, z_index * group_rows, group_rows, 0)
    logits = jnp.dot(head_rows, head_cols, preferred_element_type=jnp.float32) * LOGIT_SCALE
    masked = jnp.where(live_mask[None, :], logits, NEG_FILL)
    top_row = jnp.max(masked, axis=1)
    shifted = jnp.where(live_mask[None, :], masked - top_row[:, None], 0.0)
    expw = jnp.where(live_mask[None, :], jnp.exp(shifted), 0.0)
    target = jnp.sum(jnp.where(row_ids[:, None] == columns[None, :], logits, 0.0), axis=1)
    row_stats = jnp.stack(
        [top_row, jnp.sum(expw, axis=1), jnp.sum(expw * shifted, axis=1), target]
    ).reshape(4, y_count, tok_rows)
    half = y_count // 2
    my_half = y_index // half
    keep = lax.dynamic_slice_in_dim(row_stats, my_half * half, half, 1)
    send = lax.dynamic_slice_in_dim(row_stats, (1 - my_half) * half, half, 1)
    got = lax.ppermute(send, "y", [(p, p ^ half) for p in range(y_count)])
    merged = merge_stats(keep, got, my_half == 0)
    width = half
    while width > 1:
        width //= 2
        my_part = (y_index // width) % 2
        keep = lax.dynamic_slice_in_dim(merged, my_part * width, width, 1)
        send = lax.dynamic_slice_in_dim(merged, (1 - my_part) * width, width, 1)
        got = lax.ppermute(send, "y", [(p, p ^ width) for p in range(y_count)])
        merged = merge_stats(keep, got, my_part == 0)
    merged = merged[:, 0]
    step = 1
    while step < kv_count:
        got = lax.ppermute(merged, "kv", [(p, p ^ step) for p in range(kv_count)])
        merged = merge_stats(merged, got, (kv_index // step) % 2 == 0)
        step *= 2
    top_all, total_all, spread_all, target_all = merged[0], merged[1], merged[2], merged[3]
    log_probs = target_all - top_all - jnp.log(total_all)
    entropies = jnp.log(total_all) - spread_all / total_all
    return (log_probs, entropies)


def solution(mesh):
    kv_size, seq_size = mesh.devices.shape
    z_size = mesh.shape["seq"] // 4 if mesh.shape["seq"] % 4 == 0 else mesh.shape["seq"]
    y_size = seq_size // z_size
    split_mesh = Mesh(mesh.devices.reshape(kv_size, z_size, y_size), ("kv", "z", "y"))
    seq = ("z", "y")
    in_specs = (
        P(seq, None),
        P(),
        P(None, "kv"),
        P(None, "kv"),
        P(None, "kv"),
        P("kv", None),
        P(),
        P(None, ("kv",) + seq),
        P(),
        P(),
        P(("kv",) + seq),
    )
    out_specs = (P(seq), P(seq))
    return jax.shard_map(local, mesh=split_mesh, in_specs=in_specs, out_specs=out_specs, check_vma=False)
```

```python
import math

import jax
import jax.numpy as jnp
from jax import lax
from jax.sharding import Mesh, PartitionSpec as P

HEAD_DIM = 64


ROPE_THETA = 10000000.0
NORM_EPS = 1e-05
NEG_FILL = -1e30
ATTN_SCALE = 0.015625
RESID_SCALE = 5.0
LOGIT_SCALE = 0.125


def rms_norm(values, gain_vec):
    return (
        values * lax.rsqrt(jnp.mean(values * values, axis=-1, keepdims=True) + NORM_EPS) * gain_vec
    )


def rotate(values, positions):
    half_dim = values.shape[-1] // 2
    inverse = jnp.exp(
        jnp.arange(half_dim, dtype=jnp.float32) * (-2.0 * math.log(ROPE_THETA) / values.shape[-1])
    )
    angles = positions.astype(jnp.float32)[:, None] * inverse[None, :]
    cos_val = jnp.cos(angles)[:, None, :]
    sine_val = jnp.sin(angles)[:, None, :]
    lower_half = values[..., :half_dim]
    upper_half = values[..., half_dim:]
    return jnp.concatenate(
        [
            lower_half * cos_val - upper_half * sine_val,
            upper_half * cos_val + lower_half * sine_val,
        ],
        axis=-1,
    )


def merge_stats(mine, other, mine_first):
    first = jnp.where(mine_first, mine, other)
    second = jnp.where(mine_first, other, mine)
    top = jnp.maximum(first[0], second[0])
    gap_a = first[0] - top
    gap_b = second[0] - top
    scale_a = jnp.exp(gap_a)
    scale_b = jnp.exp(gap_b)
    total = first[1] * scale_a + second[1] * scale_b
    spread = scale_a * (first[2] + gap_a * first[1]) + scale_b * (second[2] + gap_b * second[1])
    target = first[3] + second[3]
    return jnp.stack([top, total, spread, target])


def local(
    hidden_states,
    attn_gain,
    w_q,
    w_k,
    w_v,
    w_o,
    final_gain,
    w_head,
    doc_lengths,
    target_ids,
    vocab_mask,
):
    tok_rows = hidden_states.shape[0]
    seq_index = lax.axis_index(("z", "y"))
    kv_local = w_k.shape[1] // HEAD_DIM
    q_local = w_q.shape[1] // HEAD_DIM
    group_size = q_local // kv_local
    key_width = kv_local * HEAD_DIM
    stream = hidden_states.astype(jnp.float32)
    normed_in = rms_norm(stream, attn_gain).astype(jnp.bfloat16)
    queries = jnp.dot(normed_in, w_q, preferred_element_type=jnp.float32)
    key_proj = jnp.dot(normed_in, w_k, preferred_element_type=jnp.float32)
    value_proj = jnp.dot(normed_in, w_v, preferred_element_type=jnp.float32)
    token_pos = seq_index * tok_rows + jnp.arange(tok_rows, dtype=jnp.int32)
    doc_ends = jnp.cumsum(doc_lengths)
    doc_starts = doc_ends - doc_lengths
    doc_start = jnp.max(
        jnp.where(doc_starts[None, :] <= token_pos[:, None], doc_starts[None, :], 0), axis=1
    )
    positions = token_pos - doc_start
    rotated_q = rotate(queries.reshape(tok_rows, q_local, HEAD_DIM), positions).astype(jnp.bfloat16)
    rotated_q = rotated_q.reshape(tok_rows, kv_local, group_size, HEAD_DIM)
    rotated_k = rotate(key_proj.reshape(tok_rows, kv_local, HEAD_DIM), positions).astype(
        jnp.bfloat16
    )
    packed = jnp.concatenate(
        [rotated_k.reshape(tok_rows, key_width), value_proj.astype(jnp.bfloat16)], axis=1
    )
    initial = (
        jnp.full((kv_local, group_size, tok_rows), NEG_FILL, jnp.float32),
        jnp.zeros((kv_local, group_size, tok_rows), jnp.float32),
        jnp.zeros((kv_local, group_size, tok_rows, HEAD_DIM), jnp.float32),
    )
    z_count = lax.psum(1, "z")
    y_count = lax.psum(1, "y")
    y_bits = y_count.bit_length() - 1
    z_pos = lax.axis_index("z")
    y_pos = lax.axis_index("y")
    plane_rows = y_count * tok_rows
    max_doc = (z_count * plane_rows) // 2
    back = min(-(-(max_doc - 1) // plane_rows), z_count - 1)
    held = packed[None]
    while held.shape[0] < back + 1:
        need = min(held.shape[0], back + 1 - held.shape[0])
        got = lax.ppermute(held[:need], "z", [(p, (p + need) % z_count) for p in range(z_count)])
        held = jnp.concatenate([got, held], axis=0)
    held = held[:, None]
    for bit in range(y_bits):
        mine_low = (y_pos >> bit) % 2 == 0
        got = lax.ppermute(held, "y", [(p, p ^ (1 << bit)) for p in range(y_count)])
        held = jnp.where(
            mine_low, jnp.concatenate([held, got], axis=1), jnp.concatenate([got, held], axis=1)
        )
    shard_rows = held.reshape(-1, packed.shape[1])
    plane_ids = (z_pos - back + jnp.arange(back + 1, dtype=jnp.int32)) % z_count
    key_pos = (plane_ids[:, None] * plane_rows + jnp.arange(plane_rows, dtype=jnp.int32)[None, :]).reshape(-1)
    row_count = shard_rows.shape[0]

    def update(current):
        top_score, totals, context_sum = current
        key_rows = shard_rows[:, :key_width].reshape(row_count, kv_local, HEAD_DIM)
        value_rows = shard_rows[:, key_width:].reshape(row_count, kv_local, HEAD_DIM)
        scores = (
            jnp.einsum("tkgd,skd->kgts", rotated_q, key_rows, preferred_element_type=jnp.float32)
            * ATTN_SCALE
        )
        allowed = (key_pos[None, :] >= doc_start[:, None]) & (
            key_pos[None, :] <= token_pos[:, None]
        )
        scores = jnp.where(allowed, scores, NEG_FILL)
        new_top = jnp.maximum(top_score, jnp.max(scores, axis=-1))
        weights = jnp.where(allowed, jnp.exp(scores - new_top[..., None]), 0.0)
        rescale = jnp.exp(top_score - new_top)
        totals = jnp.sum(weights, axis=-1)
        context_sum = jnp.einsum(
            "kgts,skd->kgtd",
            weights.astype(jnp.bfloat16),
            value_rows,
            preferred_element_type=jnp.float32,
        )
        return (new_top, totals, context_sum)

    top_score, totals, context_sum = update(initial)
    context = (
        (context_sum / totals[..., None])
        .transpose(2, 0, 1, 3)
        .reshape(tok_rows, q_local * HEAD_DIM)
        .astype(jnp.bfloat16)
    )
    vocab_local = w_head.shape[1]
    z_index = lax.axis_index("z")
    y_index = lax.axis_index("y")
    kv_index = lax.axis_index("kv")
    kv_count = lax.psum(1, "kv")
    kv_bits = kv_count.bit_length() - 1
    partial = jnp.dot(context, w_o, preferred_element_type=jnp.float32)
    chunk = tok_rows // kv_count
    blocks = partial.reshape((2,) * kv_bits + (chunk, partial.shape[1]))
    for bit in range(kv_bits):
        mine_low = (kv_index >> bit) % 2 == 0
        axis = kv_bits - 1 - bit
        low = lax.index_in_dim(blocks, 0, axis, keepdims=False)
        high = lax.index_in_dim(blocks, 1, axis, keepdims=False)
        keep = jnp.where(mine_low, low, high)
        send = jnp.where(mine_low, high, low)
        got = lax.ppermute(send, "kv", [(p, p ^ (1 << bit)) for p in range(kv_count)])
        blocks = jnp.where(mine_low, keep + got, got + keep)
    attn_part = blocks
    stream_part = lax.dynamic_slice_in_dim(stream, kv_index * chunk, chunk, 0)
    final_part = rms_norm(stream_part + RESID_SCALE * attn_part, final_gain).astype(jnp.bfloat16)
    y_bits = y_count.bit_length() - 1
    head_rows = final_part.reshape((1,) * (y_bits + kv_bits) + final_part.shape)
    order = [("y", bit, y_index, y_count, y_bits - 1 - bit) for bit in range(y_bits)]
    order += [("kv", bit, kv_index, kv_count, y_bits + kv_bits - 1 - bit) for bit in reversed(range(kv_bits))]
    for name, bit, pos, count, axis in order:
        mine_low = (pos >> bit) % 2 == 0
        got = lax.ppermute(head_rows, name, [(p, p ^ (1 << bit)) for p in range(count)])
        head_rows = jnp.where(
            mine_low,
            jnp.concatenate([head_rows, got], axis=axis),
            jnp.concatenate([got, head_rows], axis=axis),
        )
    head_rows = head_rows.reshape(-1, final_part.shape[1])
    group_rows = head_rows.shape[0]
    padded_local = -(-vocab_local // 16) * 16
    head_pad = jnp.zeros((16 - 1, vocab_local), w_head.dtype)
    head_ext = jnp.concatenate([w_head, vocab_mask.astype(w_head.dtype)[None, :], head_pad], axis=0)
    head_ext = jnp.pad(head_ext, ((0, 0), (0, padded_local - vocab_local)))
    head_ext = lax.all_gather(head_ext, "z", axis=1, tiled=True)
    head_cols = head_ext[: w_head.shape[0]]
    mask_cols = head_ext[w_head.shape[0]]
    live_mask = mask_cols == 1.0
    shard_ids = kv_index * (z_count * y_count) + jnp.arange(z_count, dtype=jnp.int32) * y_count + y_index
    local_cols = jnp.arange(padded_local, dtype=jnp.int32)
    columns = jnp.where(
        local_cols[None, :] < vocab_local, shard_ids[:, None] * vocab_local + local_cols[None, :], -1
    ).reshape(-1)
    row_ids = lax.dynamic_slice_in_dim(target_ids, z_index * group_rows, group_rows, 0)
    logits = jnp.dot(head_rows, head_cols, preferred_element_type=jnp.float32) * LOGIT_SCALE
    masked = jnp.where(live_mask[None, :], logits, NEG_FILL)
    top_row = jnp.max(masked, axis=1)
    shifted = jnp.where(live_mask[None, :], masked - top_row[:, None], 0.0)
    expw = jnp.where(live_mask[None, :], jnp.exp(shifted), 0.0)
    target = jnp.sum(jnp.where(row_ids[:, None] == columns[None, :], logits, 0.0), axis=1)
    row_stats = jnp.stack(
        [top_row, jnp.sum(expw, axis=1), jnp.sum(expw * shifted, axis=1), target]
    ).reshape(4, y_count, tok_rows)
    half = y_count // 2
    my_half = y_index // half
    keep = lax.dynamic_slice_in_dim(row_stats, my_half * half, half, 1)
    send = lax.dynamic_slice_in_dim(row_stats, (1 - my_half) * half, half, 1)
    got = lax.ppermute(send, "y", [(p, p ^ half) for p in range(y_count)])
    merged = merge_stats(keep, got, my_half == 0)
    width = half
    while width > 1:
        width //= 2
        my_part = (y_index // width) % 2
        keep = lax.dynamic_slice_in_dim(merged, my_part * width, width, 1)
        send = lax.dynamic_slice_in_dim(merged, (1 - my_part) * width, width, 1)
        got = lax.ppermute(send, "y", [(p, p ^ width) for p in range(y_count)])
        merged = merge_stats(keep, got, my_part == 0)
    merged = merged[:, 0]
    step = 1
    while step < kv_count:
        got = lax.ppermute(merged, "kv", [(p, p ^ step) for p in range(kv_count)])
        merged = merge_stats(merged, got, (kv_index // step) % 2 == 0)
        step *= 2
    top_all, total_all, spread_all, target_all = merged[0], merged[1], merged[2], merged[3]
    log_probs = target_all - top_all - jnp.log(total_all)
    entropies = jnp.log(total_all) - spread_all / total_all
    return (log_probs, entropies)


def solution(mesh):
    kv_size, seq_size = mesh.devices.shape
    z_size = mesh.shape["seq"] // 4 if mesh.shape["seq"] % 4 == 0 else mesh.shape["seq"]
    y_size = seq_size // z_size
    split_mesh = Mesh(mesh.devices.reshape(kv_size, z_size, y_size), ("kv", "z", "y"))
    seq = ("z", "y")
    in_specs = (
        P(seq, None),
        P(),
        P(None, "kv"),
        P(None, "kv"),
        P(None, "kv"),
        P("kv", None),
        P(),
        P(None, ("kv",) + seq),
        P(),
        P(),
        P(("kv",) + seq),
    )
    out_specs = (P(seq), P(seq))
    return jax.shard_map(local, mesh=split_mesh, in_specs=in_specs, out_specs=out_specs, check_vma=False)
```

```python
import math

import jax
import jax.numpy as jnp
from jax import lax
from jax.sharding import Mesh, PartitionSpec as P

HEAD_DIM = 64


ROPE_THETA = 10000000.0
NORM_EPS = 1e-05
NEG_FILL = -1e30
ATTN_SCALE = 0.015625
RESID_SCALE = 5.0
LOGIT_SCALE = 0.125


def rms_norm(values, gain_vec):
    return (
        values * lax.rsqrt(jnp.mean(values * values, axis=-1, keepdims=True) + NORM_EPS) * gain_vec
    )


def rotate(values, positions):
    half_dim = values.shape[-1] // 2
    inverse = jnp.exp(
        jnp.arange(half_dim, dtype=jnp.float32) * (-2.0 * math.log(ROPE_THETA) / values.shape[-1])
    )
    angles = positions.astype(jnp.float32)[:, None] * inverse[None, :]
    cos_val = jnp.cos(angles)[:, None, :]
    sine_val = jnp.sin(angles)[:, None, :]
    lower_half = values[..., :half_dim]
    upper_half = values[..., half_dim:]
    return jnp.concatenate(
        [
            lower_half * cos_val - upper_half * sine_val,
            upper_half * cos_val + lower_half * sine_val,
        ],
        axis=-1,
    )


def merge_stats(mine, other, mine_first):
    first = jnp.where(mine_first, mine, other)
    second = jnp.where(mine_first, other, mine)
    top = jnp.maximum(first[0], second[0])
    gap_a = first[0] - top
    gap_b = second[0] - top
    scale_a = jnp.exp(gap_a)
    scale_b = jnp.exp(gap_b)
    total = first[1] * scale_a + second[1] * scale_b
    spread = scale_a * (first[2] + gap_a * first[1]) + scale_b * (second[2] + gap_b * second[1])
    target = first[3] + second[3]
    return jnp.stack([top, total, spread, target])


def local(
    hidden_states,
    attn_gain,
    w_q,
    w_k,
    w_v,
    w_o,
    final_gain,
    w_head,
    doc_lengths,
    target_ids,
    vocab_mask,
):
    tok_rows = hidden_states.shape[0]
    seq_index = lax.axis_index(("z", "y"))
    kv_local = w_k.shape[1] // HEAD_DIM
    q_local = w_q.shape[1] // HEAD_DIM
    group_size = q_local // kv_local
    key_width = kv_local * HEAD_DIM
    stream = hidden_states.astype(jnp.float32)
    normed_in = rms_norm(stream, attn_gain).astype(jnp.bfloat16)
    queries = jnp.dot(normed_in, w_q, preferred_element_type=jnp.float32)
    key_proj = jnp.dot(normed_in, w_k, preferred_element_type=jnp.float32)
    value_proj = jnp.dot(normed_in, w_v, preferred_element_type=jnp.float32)
    token_pos = seq_index * tok_rows + jnp.arange(tok_rows, dtype=jnp.int32)
    doc_ends = jnp.cumsum(doc_lengths)
    doc_starts = doc_ends - doc_lengths
    doc_start = jnp.max(
        jnp.where(doc_starts[None, :] <= token_pos[:, None], doc_starts[None, :], 0), axis=1
    )
    positions = token_pos - doc_start
    rotated_q = rotate(queries.reshape(tok_rows, q_local, HEAD_DIM), positions).astype(jnp.bfloat16)
    rotated_q = rotated_q.reshape(tok_rows, kv_local, group_size, HEAD_DIM)
    rotated_k = rotate(key_proj.reshape(tok_rows, kv_local, HEAD_DIM), positions).astype(
        jnp.bfloat16
    )
    packed = jnp.concatenate(
        [rotated_k.reshape(tok_rows, key_width), value_proj.astype(jnp.bfloat16)], axis=1
    )
    initial = (
        jnp.full((kv_local, group_size, tok_rows), NEG_FILL, jnp.float32),
        jnp.zeros((kv_local, group_size, tok_rows), jnp.float32),
        jnp.zeros((kv_local, group_size, tok_rows, HEAD_DIM), jnp.float32),
    )
    z_count = lax.psum(1, "z")
    y_count = lax.psum(1, "y")
    y_bits = y_count.bit_length() - 1
    z_pos = lax.axis_index("z")
    y_pos = lax.axis_index("y")
    plane_rows = y_count * tok_rows
    max_doc = (z_count * plane_rows) // 2
    back = min(-(-(max_doc - 1) // plane_rows), z_count - 1)
    held = packed[None]
    while held.shape[0] < back + 1:
        need = min(held.shape[0], back + 1 - held.shape[0])
        got = lax.ppermute(held[:need], "z", [(p, (p + need) % z_count) for p in range(z_count)])
        held = jnp.concatenate([got, held], axis=0)
    held = held[:, None]
    for bit in range(y_bits):
        mine_low = (y_pos >> bit) % 2 == 0
        got = lax.ppermute(held, "y", [(p, p ^ (1 << bit)) for p in range(y_count)])
        held = jnp.where(
            mine_low, jnp.concatenate([held, got], axis=1), jnp.concatenate([got, held], axis=1)
        )
    shard_rows = held.reshape(-1, packed.shape[1])
    plane_ids = (z_pos - back + jnp.arange(back + 1, dtype=jnp.int32)) % z_count
    key_pos = (plane_ids[:, None] * plane_rows + jnp.arange(plane_rows, dtype=jnp.int32)[None, :]).reshape(-1)
    row_count = shard_rows.shape[0]

    def update(current):
        top_score, totals, context_sum = current
        key_rows = shard_rows[:, :key_width].reshape(row_count, kv_local, HEAD_DIM)
        value_rows = shard_rows[:, key_width:].reshape(row_count, kv_local, HEAD_DIM)
        scores = (
            jnp.einsum("tkgd,skd->kgts", rotated_q, key_rows, preferred_element_type=jnp.float32)
            * ATTN_SCALE
        )
        allowed = (key_pos[None, :] >= doc_start[:, None]) & (
            key_pos[None, :] <= token_pos[:, None]
        )
        scores = jnp.where(allowed, scores, NEG_FILL)
        new_top = jnp.maximum(top_score, jnp.max(scores, axis=-1))
        weights = jnp.where(allowed, jnp.exp(scores - new_top[..., None]), 0.0)
        rescale = jnp.exp(top_score - new_top)
        totals = jnp.sum(weights, axis=-1)
        context_sum = jnp.einsum(
            "kgts,skd->kgtd",
            weights.astype(jnp.bfloat16),
            value_rows,
            preferred_element_type=jnp.float32,
        )
        return (new_top, totals, context_sum)

    top_score, totals, context_sum = update(initial)
    context = (
        (context_sum / totals[..., None])
        .transpose(2, 0, 1, 3)
        .reshape(tok_rows, q_local * HEAD_DIM)
        .astype(jnp.bfloat16)
    )
    vocab_local = w_head.shape[1]
    z_index = lax.axis_index("z")
    y_index = lax.axis_index("y")
    kv_index = lax.axis_index("kv")
    kv_count = lax.psum(1, "kv")
    kv_bits = kv_count.bit_length() - 1
    partial = jnp.dot(context, w_o, preferred_element_type=jnp.float32)
    chunk = tok_rows // kv_count
    blocks = partial.reshape((2,) * kv_bits + (chunk, partial.shape[1]))
    for bit in range(kv_bits):
        mine_low = (kv_index >> bit) % 2 == 0
        axis = kv_bits - 1 - bit
        low = lax.index_in_dim(blocks, 0, axis, keepdims=False)
        high = lax.index_in_dim(blocks, 1, axis, keepdims=False)
        keep = jnp.where(mine_low, low, high)
        send = jnp.where(mine_low, high, low)
        got = lax.ppermute(send, "kv", [(p, p ^ (1 << bit)) for p in range(kv_count)])
        blocks = jnp.where(mine_low, keep + got, got + keep)
    attn_part = blocks
    stream_part = lax.dynamic_slice_in_dim(stream, kv_index * chunk, chunk, 0)
    final_part = rms_norm(stream_part + RESID_SCALE * attn_part, final_gain).astype(jnp.bfloat16)
    y_bits = y_count.bit_length() - 1
    head_rows = final_part.reshape((1,) * (y_bits + kv_bits) + final_part.shape)
    order = [("y", bit, y_index, y_count, y_bits - 1 - bit) for bit in range(y_bits)]
    order += [("kv", bit, kv_index, kv_count, y_bits + kv_bits - 1 - bit) for bit in reversed(range(kv_bits))]
    for name, bit, pos, count, axis in order:
        mine_low = (pos >> bit) % 2 == 0
        got = lax.ppermute(head_rows, name, [(p, p ^ (1 << bit)) for p in range(count)])
        head_rows = jnp.where(
            mine_low,
            jnp.concatenate([head_rows, got], axis=axis),
            jnp.concatenate([got, head_rows], axis=axis),
        )
    head_rows = head_rows.reshape(-1, final_part.shape[1])
    group_rows = head_rows.shape[0]
    padded_local = -(-vocab_local // 16) * 16
    head_pad = jnp.zeros((16 - 1, vocab_local), w_head.dtype)
    head_ext = jnp.concatenate([w_head, vocab_mask.astype(w_head.dtype)[None, :], head_pad], axis=0)
    head_ext = jnp.pad(head_ext, ((0, 0), (0, padded_local - vocab_local)))
    ahead = head_ext
    behind = head_ext
    ring = [head_ext]
    offsets = [0]
    for step in range(1, z_count // 2):
        ahead = lax.ppermute(ahead, "z", [(p, (p + 1) % z_count) for p in range(z_count)])
        behind = lax.ppermute(behind, "z", [(p, (p - 1) % z_count) for p in range(z_count)])
        ring += [ahead, behind]
        offsets += [-step, step]
    if z_count % 2 == 0 and z_count > 1:
        split = 1024
        top = lax.ppermute(ahead[:split], "z", [(p, (p + 1) % z_count) for p in range(z_count)])
        bottom = lax.ppermute(behind[split:], "z", [(p, (p - 1) % z_count) for p in range(z_count)])
        ring.append(jnp.concatenate([top, bottom], axis=0))
        offsets.append(z_count // 2)
    head_ext = jnp.concatenate(ring, axis=1)
    ring_z = (z_index + jnp.array(offsets, dtype=jnp.int32)) % z_count
    head_cols = head_ext[: w_head.shape[0]]
    mask_cols = head_ext[w_head.shape[0]]
    live_mask = mask_cols == 1.0
    shard_ids = kv_index * (z_count * y_count) + ring_z * y_count + y_index
    local_cols = jnp.arange(padded_local, dtype=jnp.int32)
    columns = jnp.where(
        local_cols[None, :] < vocab_local, shard_ids[:, None] * vocab_local + local_cols[None, :], -1
    ).reshape(-1)
    row_ids = lax.dynamic_slice_in_dim(target_ids, z_index * group_rows, group_rows, 0)
    logits = jnp.dot(head_rows, head_cols, preferred_element_type=jnp.float32) * LOGIT_SCALE
    masked = jnp.where(live_mask[None, :], logits, NEG_FILL)
    top_row = jnp.max(masked, axis=1)
    shifted = jnp.where(live_mask[None, :], masked - top_row[:, None], 0.0)
    expw = jnp.where(live_mask[None, :], jnp.exp(shifted), 0.0)
    target = jnp.sum(jnp.where(row_ids[:, None] == columns[None, :], logits, 0.0), axis=1)
    row_stats = jnp.stack(
        [top_row, jnp.sum(expw, axis=1), jnp.sum(expw * shifted, axis=1), target]
    ).reshape(4, y_count, tok_rows)
    half = y_count // 2
    my_half = y_index // half
    keep = lax.dynamic_slice_in_dim(row_stats, my_half * half, half, 1)
    send = lax.dynamic_slice_in_dim(row_stats, (1 - my_half) * half, half, 1)
    got = lax.ppermute(send, "y", [(p, p ^ half) for p in range(y_count)])
    merged = merge_stats(keep, got, my_half == 0)
    width = half
    while width > 1:
        width //= 2
        my_part = (y_index // width) % 2
        keep = lax.dynamic_slice_in_dim(merged, my_part * width, width, 1)
        send = lax.dynamic_slice_in_dim(merged, (1 - my_part) * width, width, 1)
        got = lax.ppermute(send, "y", [(p, p ^ width) for p in range(y_count)])
        merged = merge_stats(keep, got, my_part == 0)
    merged = merged[:, 0]
    step = 1
    while step < kv_count:
        got = lax.ppermute(merged, "kv", [(p, p ^ step) for p in range(kv_count)])
        merged = merge_stats(merged, got, (kv_index // step) % 2 == 0)
        step *= 2
    top_all, total_all, spread_all, target_all = merged[0], merged[1], merged[2], merged[3]
    log_probs = target_all - top_all - jnp.log(total_all)
    entropies = jnp.log(total_all) - spread_all / total_all
    return (log_probs, entropies)


def solution(mesh):
    kv_size, seq_size = mesh.devices.shape
    z_size = mesh.shape["seq"] // 4 if mesh.shape["seq"] % 4 == 0 else mesh.shape["seq"]
    y_size = seq_size // z_size
    split_mesh = Mesh(mesh.devices.reshape(kv_size, z_size, y_size), ("kv", "z", "y"))
    seq = ("z", "y")
    in_specs = (
        P(seq, None),
        P(),
        P(None, "kv"),
        P(None, "kv"),
        P(None, "kv"),
        P("kv", None),
        P(),
        P(None, ("kv",) + seq),
        P(),
        P(),
        P(("kv",) + seq),
    )
    out_specs = (P(seq), P(seq))
    return jax.shard_map(local, mesh=split_mesh, in_specs=in_specs, out_specs=out_specs, check_vma=False)
```

```python
import math

import jax
import jax.numpy as jnp
from jax import lax
from jax.sharding import Mesh, PartitionSpec as P

HEAD_DIM = 64


ROPE_THETA = 10000000.0
NORM_EPS = 1e-05
NEG_FILL = -1e30
ATTN_SCALE = 0.015625
RESID_SCALE = 5.0
LOGIT_SCALE = 0.125


def rms_norm(values, gain_vec):
    return (
        values * lax.rsqrt(jnp.mean(values * values, axis=-1, keepdims=True) + NORM_EPS) * gain_vec
    )


def rotate(values, positions):
    half_dim = values.shape[-1] // 2
    inverse = jnp.exp(
        jnp.arange(half_dim, dtype=jnp.float32) * (-2.0 * math.log(ROPE_THETA) / values.shape[-1])
    )
    angles = positions.astype(jnp.float32)[:, None] * inverse[None, :]
    cos_val = jnp.cos(angles)[:, None, :]
    sine_val = jnp.sin(angles)[:, None, :]
    lower_half = values[..., :half_dim]
    upper_half = values[..., half_dim:]
    return jnp.concatenate(
        [
            lower_half * cos_val - upper_half * sine_val,
            upper_half * cos_val + lower_half * sine_val,
        ],
        axis=-1,
    )


def merge_stats(mine, other, mine_first):
    first = jnp.where(mine_first, mine, other)
    second = jnp.where(mine_first, other, mine)
    top = jnp.maximum(first[0], second[0])
    gap_a = first[0] - top
    gap_b = second[0] - top
    scale_a = jnp.exp(gap_a)
    scale_b = jnp.exp(gap_b)
    total = first[1] * scale_a + second[1] * scale_b
    spread = scale_a * (first[2] + gap_a * first[1]) + scale_b * (second[2] + gap_b * second[1])
    target = first[3] + second[3]
    return jnp.stack([top, total, spread, target])


def local(
    hidden_states,
    attn_gain,
    w_q,
    w_k,
    w_v,
    w_o,
    final_gain,
    w_head,
    doc_lengths,
    target_ids,
    vocab_mask,
):
    tok_rows = hidden_states.shape[0]
    seq_index = lax.axis_index(("z", "y"))
    kv_local = w_k.shape[1] // HEAD_DIM
    q_local = w_q.shape[1] // HEAD_DIM
    group_size = q_local // kv_local
    key_width = kv_local * HEAD_DIM
    stream = hidden_states.astype(jnp.float32)
    vocab_local = w_head.shape[1]
    z_count = lax.psum(1, "z")
    z_index = lax.axis_index("z")
    padded_local = -(-vocab_local // 16) * 16
    head_pad = jnp.zeros((16 - 1, vocab_local), w_head.dtype)
    head_ext = jnp.concatenate([w_head, vocab_mask.astype(w_head.dtype)[None, :], head_pad], axis=0)
    head_ext = jnp.pad(head_ext, ((0, 0), (0, padded_local - vocab_local)))
    forward = [(p, (p + 1) % z_count) for p in range(z_count)]
    backward = [(p, (p - 1) % z_count) for p in range(z_count)]
    ring_steps = z_count // 2
    ahead = lax.ppermute(head_ext, "z", forward)
    behind = lax.ppermute(head_ext, "z", backward)
    ring = [head_ext, ahead, behind]
    offsets = [0, -1, 1]
    normed_in = rms_norm(stream, attn_gain).astype(jnp.bfloat16)
    queries = jnp.dot(normed_in, w_q, preferred_element_type=jnp.float32)
    key_proj = jnp.dot(normed_in, w_k, preferred_element_type=jnp.float32)
    value_proj = jnp.dot(normed_in, w_v, preferred_element_type=jnp.float32)
    token_pos = seq_index * tok_rows + jnp.arange(tok_rows, dtype=jnp.int32)
    doc_ends = jnp.cumsum(doc_lengths)
    doc_starts = doc_ends - doc_lengths
    doc_start = jnp.max(
        jnp.where(doc_starts[None, :] <= token_pos[:, None], doc_starts[None, :], 0), axis=1
    )
    positions = token_pos - doc_start
    rotated_q = rotate(queries.reshape(tok_rows, q_local, HEAD_DIM), positions).astype(jnp.bfloat16)
    rotated_q = rotated_q.reshape(tok_rows, kv_local, group_size, HEAD_DIM)
    rotated_k = rotate(key_proj.reshape(tok_rows, kv_local, HEAD_DIM), positions).astype(
        jnp.bfloat16
    )
    packed = jnp.concatenate(
        [rotated_k.reshape(tok_rows, key_width), value_proj.astype(jnp.bfloat16)], axis=1
    )
    initial = (
        jnp.full((kv_local, group_size, tok_rows), NEG_FILL, jnp.float32),
        jnp.zeros((kv_local, group_size, tok_rows), jnp.float32),
        jnp.zeros((kv_local, group_size, tok_rows, HEAD_DIM), jnp.float32),
    )
    z_count = lax.psum(1, "z")
    y_count = lax.psum(1, "y")
    y_bits = y_count.bit_length() - 1
    z_pos = lax.axis_index("z")
    y_pos = lax.axis_index("y")
    plane_rows = y_count * tok_rows
    max_doc = (z_count * plane_rows) // 2
    back = min(-(-(max_doc - 1) // plane_rows), z_count - 1)
    held = packed[None]
    while held.shape[0] < back + 1:
        need = min(held.shape[0], back + 1 - held.shape[0])
        got = lax.ppermute(held[:need], "z", [(p, (p + need) % z_count) for p in range(z_count)])
        held = jnp.concatenate([got, held], axis=0)
    held = held[:, None]
    for bit in range(y_bits):
        mine_low = (y_pos >> bit) % 2 == 0
        got = lax.ppermute(held, "y", [(p, p ^ (1 << bit)) for p in range(y_count)])
        held = jnp.where(
            mine_low, jnp.concatenate([held, got], axis=1), jnp.concatenate([got, held], axis=1)
        )
    shard_rows = held.reshape(-1, packed.shape[1])
    shard_rows, ahead, behind = lax.optimization_barrier((shard_rows, ahead, behind))
    ahead = lax.ppermute(ahead, "z", forward)
    behind = lax.ppermute(behind, "z", backward)
    ring += [ahead, behind]
    offsets += [-2, 2]
    plane_ids = (z_pos - back + jnp.arange(back + 1, dtype=jnp.int32)) % z_count
    key_pos = (plane_ids[:, None] * plane_rows + jnp.arange(plane_rows, dtype=jnp.int32)[None, :]).reshape(-1)
    row_count = shard_rows.shape[0]

    def update(current):
        top_score, totals, context_sum = current
        key_rows = shard_rows[:, :key_width].reshape(row_count, kv_local, HEAD_DIM)
        value_rows = shard_rows[:, key_width:].reshape(row_count, kv_local, HEAD_DIM)
        scores = (
            jnp.einsum("tkgd,skd->kgts", rotated_q, key_rows, preferred_element_type=jnp.float32)
            * ATTN_SCALE
        )
        allowed = (key_pos[None, :] >= doc_start[:, None]) & (
            key_pos[None, :] <= token_pos[:, None]
        )
        scores = jnp.where(allowed, scores, NEG_FILL)
        new_top = jnp.maximum(top_score, jnp.max(scores, axis=-1))
        weights = jnp.where(allowed, jnp.exp(scores - new_top[..., None]), 0.0)
        rescale = jnp.exp(top_score - new_top)
        totals = jnp.sum(weights, axis=-1)
        context_sum = jnp.einsum(
            "kgts,skd->kgtd",
            weights.astype(jnp.bfloat16),
            value_rows,
            preferred_element_type=jnp.float32,
        )
        return (new_top, totals, context_sum)

    top_score, totals, context_sum = update(initial)
    context_sum, ahead, behind = lax.optimization_barrier((context_sum, ahead, behind))
    ahead = lax.ppermute(ahead, "z", forward)
    behind = lax.ppermute(behind, "z", backward)
    ring += [ahead, behind]
    offsets += [-3, 3]
    context = (
        (context_sum / totals[..., None])
        .transpose(2, 0, 1, 3)
        .reshape(tok_rows, q_local * HEAD_DIM)
        .astype(jnp.bfloat16)
    )
    z_index = lax.axis_index("z")
    y_index = lax.axis_index("y")
    kv_index = lax.axis_index("kv")
    kv_count = lax.psum(1, "kv")
    kv_bits = kv_count.bit_length() - 1
    partial = jnp.dot(context, w_o, preferred_element_type=jnp.float32)
    chunk = tok_rows // kv_count
    blocks = partial.reshape((2,) * kv_bits + (chunk, partial.shape[1]))
    for bit in range(kv_bits):
        mine_low = (kv_index >> bit) % 2 == 0
        axis = kv_bits - 1 - bit
        low = lax.index_in_dim(blocks, 0, axis, keepdims=False)
        high = lax.index_in_dim(blocks, 1, axis, keepdims=False)
        keep = jnp.where(mine_low, low, high)
        send = jnp.where(mine_low, high, low)
        got = lax.ppermute(send, "kv", [(p, p ^ (1 << bit)) for p in range(kv_count)])
        blocks = jnp.where(mine_low, keep + got, got + keep)
    attn_part = blocks
    attn_part, ahead, behind = lax.optimization_barrier((attn_part, ahead, behind))
    split = 1024
    top = lax.ppermute(ahead[:split], "z", forward)
    bottom = lax.ppermute(behind[split:], "z", backward)
    ring.append(jnp.concatenate([top, bottom], axis=0))
    offsets.append(ring_steps)
    head_ext = jnp.concatenate(ring, axis=1)
    ring_z = (z_index + jnp.array(offsets, dtype=jnp.int32)) % z_count
    head_cols = head_ext[: w_head.shape[0]]
    mask_cols = head_ext[w_head.shape[0]]
    stream_part = lax.dynamic_slice_in_dim(stream, kv_index * chunk, chunk, 0)
    final_part = rms_norm(stream_part + RESID_SCALE * attn_part, final_gain).astype(jnp.bfloat16)
    y_bits = y_count.bit_length() - 1
    head_rows = final_part.reshape((1,) * (y_bits + kv_bits) + final_part.shape)
    order = [("y", bit, y_index, y_count, y_bits - 1 - bit) for bit in range(y_bits)]
    order += [("kv", bit, kv_index, kv_count, y_bits + kv_bits - 1 - bit) for bit in reversed(range(kv_bits))]
    for name, bit, pos, count, axis in order:
        mine_low = (pos >> bit) % 2 == 0
        got = lax.ppermute(head_rows, name, [(p, p ^ (1 << bit)) for p in range(count)])
        head_rows = jnp.where(
            mine_low,
            jnp.concatenate([head_rows, got], axis=axis),
            jnp.concatenate([got, head_rows], axis=axis),
        )
    head_rows = head_rows.reshape(-1, final_part.shape[1])
    group_rows = head_rows.shape[0]
    live_mask = mask_cols == 1.0
    shard_ids = kv_index * (z_count * y_count) + ring_z * y_count + y_index
    local_cols = jnp.arange(padded_local, dtype=jnp.int32)
    columns = jnp.where(
        local_cols[None, :] < vocab_local, shard_ids[:, None] * vocab_local + local_cols[None, :], -1
    ).reshape(-1)
    row_ids = lax.dynamic_slice_in_dim(target_ids, z_index * group_rows, group_rows, 0)
    logits = jnp.dot(head_rows, head_cols, preferred_element_type=jnp.float32) * LOGIT_SCALE
    masked = jnp.where(live_mask[None, :], logits, NEG_FILL)
    top_row = jnp.max(masked, axis=1)
    shifted = jnp.where(live_mask[None, :], masked - top_row[:, None], 0.0)
    expw = jnp.where(live_mask[None, :], jnp.exp(shifted), 0.0)
    target = jnp.sum(jnp.where(row_ids[:, None] == columns[None, :], logits, 0.0), axis=1)
    row_stats = jnp.stack(
        [top_row, jnp.sum(expw, axis=1), jnp.sum(expw * shifted, axis=1), target]
    ).reshape(4, y_count, tok_rows)
    half = y_count // 2
    my_half = y_index // half
    keep = lax.dynamic_slice_in_dim(row_stats, my_half * half, half, 1)
    send = lax.dynamic_slice_in_dim(row_stats, (1 - my_half) * half, half, 1)
    got = lax.ppermute(send, "y", [(p, p ^ half) for p in range(y_count)])
    merged = merge_stats(keep, got, my_half == 0)
    width = half
    while width > 1:
        width //= 2
        my_part = (y_index // width) % 2
        keep = lax.dynamic_slice_in_dim(merged, my_part * width, width, 1)
        send = lax.dynamic_slice_in_dim(merged, (1 - my_part) * width, width, 1)
        got = lax.ppermute(send, "y", [(p, p ^ width) for p in range(y_count)])
        merged = merge_stats(keep, got, my_part == 0)
    merged = merged[:, 0]
    step = 1
    while step < kv_count:
        got = lax.ppermute(merged, "kv", [(p, p ^ step) for p in range(kv_count)])
        merged = merge_stats(merged, got, (kv_index // step) % 2 == 0)
        step *= 2
    top_all, total_all, spread_all, target_all = merged[0], merged[1], merged[2], merged[3]
    log_probs = target_all - top_all - jnp.log(total_all)
    entropies = jnp.log(total_all) - spread_all / total_all
    return (log_probs, entropies)


def solution(mesh):
    kv_size, seq_size = mesh.devices.shape
    z_size = mesh.shape["seq"] // 4 if mesh.shape["seq"] % 4 == 0 else mesh.shape["seq"]
    y_size = seq_size // z_size
    split_mesh = Mesh(mesh.devices.reshape(kv_size, z_size, y_size), ("kv", "z", "y"))
    seq = ("z", "y")
    in_specs = (
        P(seq, None),
        P(),
        P(None, "kv"),
        P(None, "kv"),
        P(None, "kv"),
        P("kv", None),
        P(),
        P(None, ("kv",) + seq),
        P(),
        P(),
        P(("kv",) + seq),
    )
    out_specs = (P(seq), P(seq))
    return jax.shard_map(local, mesh=split_mesh, in_specs=in_specs, out_specs=out_specs, check_vma=False)
```

```python
import math

import jax
import jax.numpy as jnp
from jax import lax
from jax.sharding import Mesh, PartitionSpec as P

HEAD_DIM = 64


ROPE_THETA = 10000000.0
NORM_EPS = 1e-05
NEG_FILL = -1e30
ATTN_SCALE = 0.015625
RESID_SCALE = 5.0
LOGIT_SCALE = 0.125


def rms_norm(values, gain_vec):
    return (
        values * lax.rsqrt(jnp.mean(values * values, axis=-1, keepdims=True) + NORM_EPS) * gain_vec
    )


def rotate(values, positions):
    half_dim = values.shape[-1] // 2
    inverse = jnp.exp(
        jnp.arange(half_dim, dtype=jnp.float32) * (-2.0 * math.log(ROPE_THETA) / values.shape[-1])
    )
    angles = positions.astype(jnp.float32)[:, None] * inverse[None, :]
    cos_val = jnp.cos(angles)[:, None, :]
    sine_val = jnp.sin(angles)[:, None, :]
    lower_half = values[..., :half_dim]
    upper_half = values[..., half_dim:]
    return jnp.concatenate(
        [
            lower_half * cos_val - upper_half * sine_val,
            upper_half * cos_val + lower_half * sine_val,
        ],
        axis=-1,
    )


def merge_stats(mine, other, mine_first):
    first = jnp.where(mine_first, mine, other)
    second = jnp.where(mine_first, other, mine)
    top = jnp.maximum(first[0], second[0])
    gap_a = first[0] - top
    gap_b = second[0] - top
    scale_a = jnp.exp(gap_a)
    scale_b = jnp.exp(gap_b)
    total = first[1] * scale_a + second[1] * scale_b
    spread = scale_a * (first[2] + gap_a * first[1]) + scale_b * (second[2] + gap_b * second[1])
    target = first[3] + second[3]
    return jnp.stack([top, total, spread, target])


def local(
    hidden_states,
    attn_gain,
    w_q,
    w_k,
    w_v,
    w_o,
    final_gain,
    w_head,
    doc_lengths,
    target_ids,
    vocab_mask,
):
    tok_rows = hidden_states.shape[0]
    seq_index = lax.axis_index(("z", "y"))
    kv_local = w_k.shape[1] // HEAD_DIM
    q_local = w_q.shape[1] // HEAD_DIM
    group_size = q_local // kv_local
    key_width = kv_local * HEAD_DIM
    stream = hidden_states.astype(jnp.float32)
    normed_in = rms_norm(stream, attn_gain).astype(jnp.bfloat16)
    queries = jnp.dot(normed_in, w_q, preferred_element_type=jnp.float32)
    key_proj = jnp.dot(normed_in, w_k, preferred_element_type=jnp.float32)
    value_proj = jnp.dot(normed_in, w_v, preferred_element_type=jnp.float32)
    token_pos = seq_index * tok_rows + jnp.arange(tok_rows, dtype=jnp.int32)
    doc_ends = jnp.cumsum(doc_lengths)
    doc_starts = doc_ends - doc_lengths
    doc_start = jnp.max(
        jnp.where(doc_starts[None, :] <= token_pos[:, None], doc_starts[None, :], 0), axis=1
    )
    positions = token_pos - doc_start
    rotated_q = rotate(queries.reshape(tok_rows, q_local, HEAD_DIM), positions).astype(jnp.bfloat16)
    rotated_q = rotated_q.reshape(tok_rows, kv_local, group_size, HEAD_DIM)
    rotated_k = rotate(key_proj.reshape(tok_rows, kv_local, HEAD_DIM), positions).astype(
        jnp.bfloat16
    )
    packed = jnp.concatenate(
        [rotated_k.reshape(tok_rows, key_width), value_proj.astype(jnp.bfloat16)], axis=1
    )
    initial = (
        jnp.full((kv_local, group_size, tok_rows), NEG_FILL, jnp.float32),
        jnp.zeros((kv_local, group_size, tok_rows), jnp.float32),
        jnp.zeros((kv_local, group_size, tok_rows, HEAD_DIM), jnp.float32),
    )
    z_count = lax.psum(1, "z")
    y_count = lax.psum(1, "y")
    y_bits = y_count.bit_length() - 1
    z_pos = lax.axis_index("z")
    y_pos = lax.axis_index("y")
    plane_rows = y_count * tok_rows
    max_doc = (z_count * plane_rows) // 2
    back = min(-(-(max_doc - 1) // plane_rows), z_count - 1)
    held = packed[None]
    while held.shape[0] < back + 1:
        need = min(held.shape[0], back + 1 - held.shape[0])
        got = lax.ppermute(held[:need], "z", [(p, (p + need) % z_count) for p in range(z_count)])
        held = jnp.concatenate([got, held], axis=0)
    padded_local = -(-w_head.shape[1] // 16) * 16
    head_pad = jnp.zeros((16 - 1, w_head.shape[1]), w_head.dtype)
    head_ext = jnp.concatenate([w_head, vocab_mask.astype(w_head.dtype)[None, :], head_pad], axis=0)
    head_ext = jnp.pad(head_ext, ((0, 0), (0, padded_local - w_head.shape[1])))
    held, head_ext = lax.optimization_barrier((held, head_ext))
    held = held[:, None]
    for bit in range(y_bits):
        mine_low = (y_pos >> bit) % 2 == 0
        got = lax.ppermute(held, "y", [(p, p ^ (1 << bit)) for p in range(y_count)])
        held = jnp.where(
            mine_low, jnp.concatenate([held, got], axis=1), jnp.concatenate([got, held], axis=1)
        )
    shard_rows = held.reshape(-1, packed.shape[1])
    plane_ids = (z_pos - back + jnp.arange(back + 1, dtype=jnp.int32)) % z_count
    key_pos = (plane_ids[:, None] * plane_rows + jnp.arange(plane_rows, dtype=jnp.int32)[None, :]).reshape(-1)
    row_count = shard_rows.shape[0]

    def update(current):
        top_score, totals, context_sum = current
        key_rows = shard_rows[:, :key_width].reshape(row_count, kv_local, HEAD_DIM)
        value_rows = shard_rows[:, key_width:].reshape(row_count, kv_local, HEAD_DIM)
        scores = (
            jnp.einsum("tkgd,skd->kgts", rotated_q, key_rows, preferred_element_type=jnp.float32)
            * ATTN_SCALE
        )
        allowed = (key_pos[None, :] >= doc_start[:, None]) & (
            key_pos[None, :] <= token_pos[:, None]
        )
        scores = jnp.where(allowed, scores, NEG_FILL)
        new_top = jnp.maximum(top_score, jnp.max(scores, axis=-1))
        weights = jnp.where(allowed, jnp.exp(scores - new_top[..., None]), 0.0)
        rescale = jnp.exp(top_score - new_top)
        totals = jnp.sum(weights, axis=-1)
        context_sum = jnp.einsum(
            "kgts,skd->kgtd",
            weights.astype(jnp.bfloat16),
            value_rows,
            preferred_element_type=jnp.float32,
        )
        return (new_top, totals, context_sum)

    top_score, totals, context_sum = update(initial)
    context = (
        (context_sum / totals[..., None])
        .transpose(2, 0, 1, 3)
        .reshape(tok_rows, q_local * HEAD_DIM)
        .astype(jnp.bfloat16)
    )
    vocab_local = w_head.shape[1]
    z_index = lax.axis_index("z")
    y_index = lax.axis_index("y")
    kv_index = lax.axis_index("kv")
    kv_count = lax.psum(1, "kv")
    kv_bits = kv_count.bit_length() - 1
    partial = jnp.dot(context, w_o, preferred_element_type=jnp.float32)
    chunk = tok_rows // kv_count
    blocks = partial.reshape((2,) * kv_bits + (chunk, partial.shape[1]))
    for bit in range(kv_bits):
        mine_low = (kv_index >> bit) % 2 == 0
        axis = kv_bits - 1 - bit
        low = lax.index_in_dim(blocks, 0, axis, keepdims=False)
        high = lax.index_in_dim(blocks, 1, axis, keepdims=False)
        keep = jnp.where(mine_low, low, high)
        send = jnp.where(mine_low, high, low)
        got = lax.ppermute(send, "kv", [(p, p ^ (1 << bit)) for p in range(kv_count)])
        blocks = jnp.where(mine_low, keep + got, got + keep)
    attn_part = blocks
    stream_part = lax.dynamic_slice_in_dim(stream, kv_index * chunk, chunk, 0)
    final_part = rms_norm(stream_part + RESID_SCALE * attn_part, final_gain).astype(jnp.bfloat16)
    y_bits = y_count.bit_length() - 1
    head_rows = final_part.reshape((1,) * (y_bits + kv_bits) + final_part.shape)
    order = [("y", bit, y_index, y_count, y_bits - 1 - bit) for bit in range(y_bits)]
    order += [("kv", bit, kv_index, kv_count, y_bits + kv_bits - 1 - bit) for bit in reversed(range(kv_bits))]
    for name, bit, pos, count, axis in order:
        mine_low = (pos >> bit) % 2 == 0
        got = lax.ppermute(head_rows, name, [(p, p ^ (1 << bit)) for p in range(count)])
        head_rows = jnp.where(
            mine_low,
            jnp.concatenate([head_rows, got], axis=axis),
            jnp.concatenate([got, head_rows], axis=axis),
        )
    head_rows = head_rows.reshape(-1, final_part.shape[1])
    group_rows = head_rows.shape[0]
    head_ext = lax.all_gather(head_ext, "z", axis=1, tiled=True)
    head_cols = head_ext[: w_head.shape[0]]
    mask_cols = head_ext[w_head.shape[0]]
    live_mask = mask_cols == 1.0
    shard_ids = kv_index * (z_count * y_count) + jnp.arange(z_count, dtype=jnp.int32) * y_count + y_index
    local_cols = jnp.arange(padded_local, dtype=jnp.int32)
    columns = jnp.where(
        local_cols[None, :] < vocab_local, shard_ids[:, None] * vocab_local + local_cols[None, :], -1
    ).reshape(-1)
    row_ids = lax.dynamic_slice_in_dim(target_ids, z_index * group_rows, group_rows, 0)
    logits = jnp.dot(head_rows, head_cols, preferred_element_type=jnp.float32) * LOGIT_SCALE
    masked = jnp.where(live_mask[None, :], logits, NEG_FILL)
    top_row = jnp.max(masked, axis=1)
    shifted = jnp.where(live_mask[None, :], masked - top_row[:, None], 0.0)
    expw = jnp.where(live_mask[None, :], jnp.exp(shifted), 0.0)
    target = jnp.sum(jnp.where(row_ids[:, None] == columns[None, :], logits, 0.0), axis=1)
    row_stats = jnp.stack(
        [top_row, jnp.sum(expw, axis=1), jnp.sum(expw * shifted, axis=1), target]
    ).reshape(4, y_count, tok_rows)
    half = y_count // 2
    my_half = y_index // half
    keep = lax.dynamic_slice_in_dim(row_stats, my_half * half, half, 1)
    send = lax.dynamic_slice_in_dim(row_stats, (1 - my_half) * half, half, 1)
    got = lax.ppermute(send, "y", [(p, p ^ half) for p in range(y_count)])
    merged = merge_stats(keep, got, my_half == 0)
    width = half
    while width > 1:
        width //= 2
        my_part = (y_index // width) % 2
        keep = lax.dynamic_slice_in_dim(merged, my_part * width, width, 1)
        send = lax.dynamic_slice_in_dim(merged, (1 - my_part) * width, width, 1)
        got = lax.ppermute(send, "y", [(p, p ^ width) for p in range(y_count)])
        merged = merge_stats(keep, got, my_part == 0)
    merged = merged[:, 0]
    step = 1
    while step < kv_count:
        got = lax.ppermute(merged, "kv", [(p, p ^ step) for p in range(kv_count)])
        merged = merge_stats(merged, got, (kv_index // step) % 2 == 0)
        step *= 2
    top_all, total_all, spread_all, target_all = merged[0], merged[1], merged[2], merged[3]
    log_probs = target_all - top_all - jnp.log(total_all)
    entropies = jnp.log(total_all) - spread_all / total_all
    return (log_probs, entropies)


def solution(mesh):
    kv_size, seq_size = mesh.devices.shape
    z_size = mesh.shape["seq"] // 4 if mesh.shape["seq"] % 4 == 0 else mesh.shape["seq"]
    y_size = seq_size // z_size
    split_mesh = Mesh(mesh.devices.reshape(kv_size, z_size, y_size), ("kv", "z", "y"))
    seq = ("z", "y")
    in_specs = (
        P(seq, None),
        P(),
        P(None, "kv"),
        P(None, "kv"),
        P(None, "kv"),
        P("kv", None),
        P(),
        P(None, ("kv",) + seq),
        P(),
        P(),
        P(("kv",) + seq),
    )
    out_specs = (P(seq), P(seq))
    return jax.shard_map(local, mesh=split_mesh, in_specs=in_specs, out_specs=out_specs, check_vma=False)
```

```python
import math

import jax
import jax.numpy as jnp
from jax import lax
from jax.sharding import Mesh, PartitionSpec as P

HEAD_DIM = 64


ROPE_THETA = 10000000.0
NORM_EPS = 1e-05
NEG_FILL = -1e30
ATTN_SCALE = 0.015625
RESID_SCALE = 5.0
LOGIT_SCALE = 0.125


def rms_norm(values, gain_vec):
    return (
        values * lax.rsqrt(jnp.mean(values * values, axis=-1, keepdims=True) + NORM_EPS) * gain_vec
    )


def rotate(values, positions):
    half_dim = values.shape[-1] // 2
    inverse = jnp.exp(
        jnp.arange(half_dim, dtype=jnp.float32) * (-2.0 * math.log(ROPE_THETA) / values.shape[-1])
    )
    angles = positions.astype(jnp.float32)[:, None] * inverse[None, :]
    cos_val = jnp.cos(angles)[:, None, :]
    sine_val = jnp.sin(angles)[:, None, :]
    lower_half = values[..., :half_dim]
    upper_half = values[..., half_dim:]
    return jnp.concatenate(
        [
            lower_half * cos_val - upper_half * sine_val,
            upper_half * cos_val + lower_half * sine_val,
        ],
        axis=-1,
    )


def merge_stats(mine, other, mine_first):
    first = jnp.where(mine_first, mine, other)
    second = jnp.where(mine_first, other, mine)
    top = jnp.maximum(first[0], second[0])
    gap_a = first[0] - top
    gap_b = second[0] - top
    scale_a = jnp.exp(gap_a)
    scale_b = jnp.exp(gap_b)
    total = first[1] * scale_a + second[1] * scale_b
    spread = scale_a * (first[2] + gap_a * first[1]) + scale_b * (second[2] + gap_b * second[1])
    target = first[3] + second[3]
    return jnp.stack([top, total, spread, target])


def local(
    hidden_states,
    attn_gain,
    w_q,
    w_k,
    w_v,
    w_o,
    final_gain,
    w_head,
    doc_lengths,
    target_ids,
    vocab_mask,
):
    tok_rows = hidden_states.shape[0]
    seq_index = lax.axis_index(("z", "y"))
    kv_local = w_k.shape[1] // HEAD_DIM
    q_local = w_q.shape[1] // HEAD_DIM
    group_size = q_local // kv_local
    key_width = kv_local * HEAD_DIM
    stream = hidden_states.astype(jnp.float32)
    normed_in = rms_norm(stream, attn_gain).astype(jnp.bfloat16)
    queries = jnp.dot(normed_in, w_q, preferred_element_type=jnp.float32)
    key_proj = jnp.dot(normed_in, w_k, preferred_element_type=jnp.float32)
    value_proj = jnp.dot(normed_in, w_v, preferred_element_type=jnp.float32)
    token_pos = seq_index * tok_rows + jnp.arange(tok_rows, dtype=jnp.int32)
    doc_ends = jnp.cumsum(doc_lengths)
    doc_starts = doc_ends - doc_lengths
    doc_start = jnp.max(
        jnp.where(doc_starts[None, :] <= token_pos[:, None], doc_starts[None, :], 0), axis=1
    )
    positions = token_pos - doc_start
    rotated_q = rotate(queries.reshape(tok_rows, q_local, HEAD_DIM), positions).astype(jnp.bfloat16)
    rotated_q = rotated_q.reshape(tok_rows, kv_local, group_size, HEAD_DIM)
    rotated_k = rotate(key_proj.reshape(tok_rows, kv_local, HEAD_DIM), positions).astype(
        jnp.bfloat16
    )
    packed = jnp.concatenate(
        [rotated_k.reshape(tok_rows, key_width), value_proj.astype(jnp.bfloat16)], axis=1
    )
    initial = (
        jnp.full((kv_local, group_size, tok_rows), NEG_FILL, jnp.float32),
        jnp.zeros((kv_local, group_size, tok_rows), jnp.float32),
        jnp.zeros((kv_local, group_size, tok_rows, HEAD_DIM), jnp.float32),
    )
    z_count = lax.psum(1, "z")
    y_count = lax.psum(1, "y")
    y_bits = y_count.bit_length() - 1
    z_pos = lax.axis_index("z")
    y_pos = lax.axis_index("y")
    plane_rows = y_count * tok_rows
    max_doc = (z_count * plane_rows) // 2
    back = min(-(-(max_doc - 1) // plane_rows), z_count - 1)
    held = packed[None]
    while held.shape[0] < back + 1:
        need = min(held.shape[0], back + 1 - held.shape[0])
        got = lax.ppermute(held[:need], "z", [(p, (p + need) % z_count) for p in range(z_count)])
        held = jnp.concatenate([got, held], axis=0)
    padded_local = -(-w_head.shape[1] // 16) * 16
    head_pad = jnp.zeros((16 - 1, w_head.shape[1]), w_head.dtype)
    head_ext = jnp.concatenate([w_head, vocab_mask.astype(w_head.dtype)[None, :], head_pad], axis=0)
    head_ext = jnp.pad(head_ext, ((0, 0), (0, padded_local - w_head.shape[1])))
    held, head_ext = lax.optimization_barrier((held, head_ext))
    held = held[:, None]
    for bit in range(y_bits):
        mine_low = (y_pos >> bit) % 2 == 0
        got = lax.ppermute(held, "y", [(p, p ^ (1 << bit)) for p in range(y_count)])
        held = jnp.where(
            mine_low, jnp.concatenate([held, got], axis=1), jnp.concatenate([got, held], axis=1)
        )
    shard_rows = held.reshape(-1, packed.shape[1])
    plane_ids = (z_pos - back + jnp.arange(back + 1, dtype=jnp.int32)) % z_count
    key_pos = (plane_ids[:, None] * plane_rows + jnp.arange(plane_rows, dtype=jnp.int32)[None, :]).reshape(-1)
    row_count = shard_rows.shape[0]

    def update(current):
        top_score, totals, context_sum = current
        key_rows = shard_rows[:, :key_width].reshape(row_count, kv_local, HEAD_DIM)
        value_rows = shard_rows[:, key_width:].reshape(row_count, kv_local, HEAD_DIM)
        scores = (
            jnp.einsum("tkgd,skd->kgts", rotated_q, key_rows, preferred_element_type=jnp.float32)
            * ATTN_SCALE
        )
        allowed = (key_pos[None, :] >= doc_start[:, None]) & (
            key_pos[None, :] <= token_pos[:, None]
        )
        scores = jnp.where(allowed, scores, NEG_FILL)
        new_top = jnp.maximum(top_score, jnp.max(scores, axis=-1))
        weights = jnp.where(allowed, jnp.exp(scores - new_top[..., None]), 0.0)
        rescale = jnp.exp(top_score - new_top)
        totals = jnp.sum(weights, axis=-1)
        context_sum = jnp.einsum(
            "kgts,skd->kgtd",
            weights.astype(jnp.bfloat16),
            value_rows,
            preferred_element_type=jnp.float32,
        )
        return (new_top, totals, context_sum)

    top_score, totals, context_sum = update(initial)
    context = (
        (context_sum / totals[..., None])
        .transpose(2, 0, 1, 3)
        .reshape(tok_rows, q_local * HEAD_DIM)
        .astype(jnp.bfloat16)
    )
    vocab_local = w_head.shape[1]
    z_index = lax.axis_index("z")
    y_index = lax.axis_index("y")
    kv_index = lax.axis_index("kv")
    kv_count = lax.psum(1, "kv")
    kv_bits = kv_count.bit_length() - 1
    partial = jnp.dot(context, w_o, preferred_element_type=jnp.float32)
    chunk = tok_rows // kv_count
    blocks = partial.reshape((2,) * kv_bits + (chunk, partial.shape[1]))
    for bit in range(kv_bits):
        mine_low = (kv_index >> bit) % 2 == 0
        axis = kv_bits - 1 - bit
        low = lax.index_in_dim(blocks, 0, axis, keepdims=False)
        high = lax.index_in_dim(blocks, 1, axis, keepdims=False)
        keep = jnp.where(mine_low, low, high)
        send = jnp.where(mine_low, high, low)
        got = lax.ppermute(send, "kv", [(p, p ^ (1 << bit)) for p in range(kv_count)])
        blocks = jnp.where(mine_low, keep + got, got + keep)
    attn_part = blocks
    stream_part = lax.dynamic_slice_in_dim(stream, kv_index * chunk, chunk, 0)
    final_part = rms_norm(stream_part + RESID_SCALE * attn_part, final_gain).astype(jnp.bfloat16)
    y_bits = y_count.bit_length() - 1
    head_rows = final_part.reshape((1,) * (y_bits + kv_bits) + final_part.shape)
    order = [("y", bit, y_index, y_count, y_bits - 1 - bit) for bit in range(y_bits)]
    order += [("kv", bit, kv_index, kv_count, y_bits + kv_bits - 1 - bit) for bit in reversed(range(kv_bits))]
    for name, bit, pos, count, axis in order:
        mine_low = (pos >> bit) % 2 == 0
        got = lax.ppermute(head_rows, name, [(p, p ^ (1 << bit)) for p in range(count)])
        if name == "kv" and bit == 0:
            head_rows = jnp.concatenate([head_rows, got], axis=axis)
        else:
            head_rows = jnp.where(
                mine_low,
                jnp.concatenate([head_rows, got], axis=axis),
                jnp.concatenate([got, head_rows], axis=axis),
            )
    head_rows = head_rows.reshape(-1, final_part.shape[1])
    pair_swapped = kv_index % 2 == 1

    def unswap(values):
        lead = values.shape[:-1]
        split = values.reshape(lead + (values.shape[-1] // (2 * chunk), 2, chunk))
        return jnp.where(pair_swapped, jnp.flip(split, axis=-2), split).reshape(values.shape)

    group_rows = head_rows.shape[0]
    head_ext = lax.all_gather(head_ext, "z", axis=1, tiled=True)
    head_cols = head_ext[: w_head.shape[0]]
    mask_cols = head_ext[w_head.shape[0]]
    live_mask = mask_cols == 1.0
    shard_ids = kv_index * (z_count * y_count) + jnp.arange(z_count, dtype=jnp.int32) * y_count + y_index
    local_cols = jnp.arange(padded_local, dtype=jnp.int32)
    columns = jnp.where(
        local_cols[None, :] < vocab_local, shard_ids[:, None] * vocab_local + local_cols[None, :], -1
    ).reshape(-1)
    row_ids = unswap(lax.dynamic_slice_in_dim(target_ids, z_index * group_rows, group_rows, 0))
    logits = jnp.dot(head_rows, head_cols, preferred_element_type=jnp.float32) * LOGIT_SCALE
    masked = jnp.where(live_mask[None, :], logits, NEG_FILL)
    top_row = jnp.max(masked, axis=1)
    shifted = jnp.where(live_mask[None, :], masked - top_row[:, None], 0.0)
    expw = jnp.where(live_mask[None, :], jnp.exp(shifted), 0.0)
    target = jnp.sum(jnp.where(row_ids[:, None] == columns[None, :], logits, 0.0), axis=1)
    row_stats = jnp.stack(
        [top_row, jnp.sum(expw, axis=1), jnp.sum(expw * shifted, axis=1), target]
    ).reshape(4, y_count, tok_rows)
    half = y_count // 2
    my_half = y_index // half
    keep = lax.dynamic_slice_in_dim(row_stats, my_half * half, half, 1)
    send = lax.dynamic_slice_in_dim(row_stats, (1 - my_half) * half, half, 1)
    got = lax.ppermute(send, "y", [(p, p ^ half) for p in range(y_count)])
    merged = merge_stats(keep, got, my_half == 0)
    width = half
    while width > 1:
        width //= 2
        my_part = (y_index // width) % 2
        keep = lax.dynamic_slice_in_dim(merged, my_part * width, width, 1)
        send = lax.dynamic_slice_in_dim(merged, (1 - my_part) * width, width, 1)
        got = lax.ppermute(send, "y", [(p, p ^ width) for p in range(y_count)])
        merged = merge_stats(keep, got, my_part == 0)
    merged = unswap(merged[:, 0])
    step = 1
    while step < kv_count:
        got = lax.ppermute(merged, "kv", [(p, p ^ step) for p in range(kv_count)])
        merged = merge_stats(merged, got, (kv_index // step) % 2 == 0)
        step *= 2
    top_all, total_all, spread_all, target_all = merged[0], merged[1], merged[2], merged[3]
    log_probs = target_all - top_all - jnp.log(total_all)
    entropies = jnp.log(total_all) - spread_all / total_all
    return (log_probs, entropies)


def solution(mesh):
    kv_size, seq_size = mesh.devices.shape
    z_size = mesh.shape["seq"] // 4 if mesh.shape["seq"] % 4 == 0 else mesh.shape["seq"]
    y_size = seq_size // z_size
    split_mesh = Mesh(mesh.devices.reshape(kv_size, z_size, y_size), ("kv", "z", "y"))
    seq = ("z", "y")
    in_specs = (
        P(seq, None),
        P(),
        P(None, "kv"),
        P(None, "kv"),
        P(None, "kv"),
        P("kv", None),
        P(),
        P(None, ("kv",) + seq),
        P(),
        P(),
        P(("kv",) + seq),
    )
    out_specs = (P(seq), P(seq))
    return jax.shard_map(local, mesh=split_mesh, in_specs=in_specs, out_specs=out_specs, check_vma=False)
```
